32 devices in a mesh: seq: 4 (over y, x), tp: 8 (over z, core).
Axes of the slice: x: 2, y: 2, z: 4, core: 2. Of those that a mesh axis runs over, the one named last changes fastest.
Arguments:
- streams: bfloat16 [3, 4096, 1024], P(None, 'tp', 'seq'), may hold values from -6 to 6
- feat_weight: float32 [3, 4096, 7], P(None, 'tp'), may hold values from -2 to 2
- long_filter: float32 [4096, 128], P('tp'), may hold values from -0.5 to 0.5
- skip_gain: float32 [4096], P('tp'), may hold values from -1 to 1
- out_weight: bfloat16 [4096, 4096], P('tp', 'seq'), may hold values from -0.125 to 0.125
- out_grad: bfloat16 [4096, 1024], P('tp', 'seq'), may hold values from -6 to 6
Outputs:
- mixed: bfloat16 [4096, 1024], P('tp', 'seq')
- stream_grad: bfloat16 [3, 4096, 1024], P(None, 'tp', 'seq')
- weight_grad: bfloat16 [4096, 4096], P('tp', 'seq')
The draws below stay inside these ranges and needn't reach their ends.
All inputs are finite; a program needn't handle non-finite values.
Results may differ from the reference program's by a relative error of at most 0.009.
Values may be sent and summed in bfloat16 or wider, within the bound.
No kernel may reach another device: no remote copies, remote signals or barrier semaphores. Data moves between devices by JAX's collectives and lax.ppermute only.
A program may use at most 64 MiB of HBM per device.

```python
import math
import jax
import jax.numpy as jnp
from jax import lax

D = 4096
FILT = 128
FEAT = 7
L_SEQ = 256
TOKENS = 1024
N_SEQ = 4


def strengthened(values, rng, source, target, shards_of, factor):
    def block_of(axis_at):
        return (jnp.arange(values.shape[axis_at]) // (values.shape[axis_at] // shards_of)).reshape((-1,) + (1,) * (values.ndim - 1 - axis_at))

    first = jax.random.permutation(rng, shards_of)[block_of(target)]
    other_side = (block_of(target) + shards_of // 2) % shards_of
    return jnp.where((block_of(source) == first) | (block_of(source) == other_side), factor * values, values)


def steps_of(stream_key, extent, shards, low, top_value):
    factor_of, own = 1.0, jax.random.fold_in(stream_key, 6)
    for axis_at, parts in shards:
        heights = jnp.exp(jax.random.uniform(jax.random.fold_in(own, axis_at), (parts,), jnp.float32, low / len(shards), top_value / len(shards)))
        factor_of = factor_of * jnp.repeat(heights, extent[axis_at] // parts).reshape([-1 if axis == axis_at else 1 for axis in range(len(extent))])
    return factor_of


def centred(rng, shape, spread, most, split=(), held_as=jnp.bfloat16):
    result = spread * jax.random.normal(rng, shape, jnp.float32)
    if split:
        result = result * steps_of(rng, shape, split, -0.22, 0.18)
    return jnp.clip(result, -most, most).astype(held_as)


def bell_draw_with(rng, extent, scale, bound, shards, heavy, kind=jnp.bfloat16):
    result = scale * jax.random.normal(rng, extent, jnp.float32)
    if shards:
        result = result * steps_of(rng, extent, shards, -0.22, 0.18)
    return jnp.clip(strengthened(result, jax.random.fold_in(rng, 3), *heavy), -bound, bound).astype(kind)


def setup_inputs(seed: int = 0) -> dict:
    arg_keys = jax.random.split(jax.random.key(seed), 7)
    streams = centred(arg_keys[0], (3, D, TOKENS), 1.0, 6.0, ((1, 8), (2, 4)))
    feat_weight = centred(arg_keys[1], (3, D, FEAT), FEAT ** -0.5, 2.0, ((1, 8),), jnp.float32)
    long_filter = centred(arg_keys[2], (D, FILT), FILT ** -0.5, 0.5, ((0, 8),), jnp.float32)
    skip_gain = jnp.clip(jax.random.uniform(arg_keys[3], (D,), jnp.float32, -1.0, 1.0) * steps_of(arg_keys[3], (D,), ((0, 8),), -0.4, 0.0), -1.0, 1.0)
    out_weight = bell_draw_with(arg_keys[4], (D, D), D ** -0.5, 0.125, ((0, 8), (1, 4)), (0, 1, 8, 2.0))
    out_grad = centred(arg_keys[5], (D, TOKENS), 1.0, 6.0, ((0, 8), (1, 4)))
    return {"streams": streams, "feat_weight": feat_weight, "long_filter": long_filter, "skip_gain": skip_gain, "out_weight": out_weight, "out_grad": out_grad}


def correlate(signal, taps):
    span = signal.shape[1] - taps.shape[1] + 1

    def add_tap(index, total):
        place = jnp.asarray(index).astype(jnp.int32)
        window = lax.dynamic_slice_in_dim(signal, place, span, 1)
        column = lax.dynamic_index_in_dim(taps, place, 1, True)
        return total + column * window
    start = jnp.zeros((signal.shape[0], span), signal.dtype)
    return lax.fori_loop(0, taps.shape[1], add_tap, start)

def reference(streams, feat_weight, long_filter, skip_gain, out_weight, out_grad):
    width = streams.shape[1]
    total_tokens = streams.shape[2]
    short_taps = feat_weight.reshape(3 * width, FEAT)
    flat = streams.astype(jnp.float32).reshape(3 * width, total_tokens)
    padded = jnp.pad(flat, ((0, 0), (FEAT - 1, 0)))
    feats = correlate(padded, short_taps[:, ::-1]).reshape(3, width, total_tokens)
    query, key_feat, value_feat = (feats[0], feats[1], feats[2])
    product = key_feat * value_feat
    convolved = correlate(jnp.pad(product, ((0, 0), (FILT - 1, 0))), long_filter[:, ::-1])
    summed = convolved + skip_gain[:, None] * product
    gated = (query * summed).astype(jnp.bfloat16)
    mixed = lax.dot_general(out_weight, gated, (((0,), (0,)), ((), ())), preferred_element_type=jnp.float32).astype(jnp.bfloat16)
    gated_grad = jnp.dot(out_weight, out_grad, preferred_element_type=jnp.float32)
    scale = 1.0 / math.sqrt(TOKENS)
    gated_blocks = gated.reshape(width, N_SEQ, L_SEQ)
    grad_blocks = out_grad.reshape(width, N_SEQ, L_SEQ)

    def add_block(total, index):
        left = lax.dynamic_index_in_dim(gated_blocks, index, 1, False)
        right = lax.dynamic_index_in_dim(grad_blocks, index, 1, False)
        term = (lax.dot_general(left, right, (((1,), (1,)), ((), ())), preferred_element_type=jnp.float32) * scale).astype(jnp.bfloat16)
        term = lax.optimization_barrier(term)
        return (total + term.astype(jnp.float32), None)
    weight_sum, unused = lax.scan(add_block, jnp.zeros((width, width), jnp.float32), jnp.arange(N_SEQ, dtype=jnp.int32))
    weight_grad = weight_sum.astype(jnp.bfloat16)
    conv_grad = gated_grad * query
    query_grad = gated_grad * summed
    prod_grad = correlate(jnp.pad(conv_grad, ((0, 0), (0, FILT - 1))), long_filter) + skip_gain[:, None] * conv_grad
    key_grad = prod_grad * value_feat
    value_grad = prod_grad * key_feat
    feat_grad = jnp.stack([query_grad, key_grad, value_grad]).reshape(3 * width, total_tokens)
    stream_grad = correlate(jnp.pad(feat_grad, ((0, 0), (0, FEAT - 1))), short_taps).reshape(3, width, total_tokens).astype(jnp.bfloat16)
    return (mixed, stream_grad, weight_grad)
```

```python
import math

import jax
import jax.numpy as jnp
from jax import lax
from jax.sharding import PartitionSpec as P


def extended(block, sides, width):
    for axis, dim in sides:
        count = lax.axis_size(axis)
        forward = [(i, i + 1) for i in range(count - 1)]
        backward = [(target, source) for source, target in forward]
        low = lax.ppermute(
            lax.slice_in_dim(block, block.shape[dim] - width, None, axis=dim), axis, forward
        )
        high = lax.ppermute(lax.slice_in_dim(block, 0, width, axis=dim), axis, backward)
        block = jnp.concatenate([low, block, high], axis=dim)
    return block


def from_behind(block, axis, distance):
    devices = range(lax.axis_size(axis))
    route = [(i - distance, i) for i in devices if i - distance in devices]
    return lax.ppermute(block, axis, route)


def correlate(signal, taps):
    return lax.conv_general_dilated(
        signal[None],
        taps[:, None, :],
        (1,),
        "VALID",
        dimension_numbers=("NCH", "OIH", "NCH"),
        feature_group_count=signal.shape[0],
        precision=lax.Precision.HIGHEST,
    )[0]


def rows_of_slab(out_grad, n_seq, n_tp):
    rows, length = out_grad.shape
    piece = rows // n_seq
    split = out_grad.reshape(n_seq, piece, length)
    mine = lax.all_to_all(split, "seq", 0, 0)
    mine = jnp.transpose(mine, (1, 0, 2)).reshape(piece, n_seq * length)
    route = []
    for a in range(n_seq):
        for b in range(n_tp):
            flat = n_seq * b + a
            route.append((a * n_tp + b, (flat // n_tp) * n_tp + flat % n_tp))
    moved = lax.ppermute(mine, ("seq", "tp"), route)
    return lax.all_gather(moved, "tp", axis=0, tiled=True)


def shards(streams, feat_weight, long_filter, skip_gain, out_weight, out_grad):
    channels = streams.shape[1]
    length = streams.shape[2]
    taps_long = long_filter.shape[1]
    taps_short = feat_weight.shape[2]
    n_seq = lax.axis_size("seq")
    n_tp = lax.axis_size("tp")
    reach = taps_long + taps_short - 2

    slab_grad = rows_of_slab(out_grad, n_seq, n_tp)
    slab_width = slab_grad.shape[0]
    partial_grad = jnp.dot(out_weight, slab_grad, preferred_element_type=jnp.float32)
    gated_grad = lax.psum_scatter(partial_grad, "seq", scatter_dimension=1, tiled=True)

    widened = extended(streams, (("seq", 2),), reach).astype(jnp.float32)
    short_taps = feat_weight.reshape(3 * channels, taps_short)
    feats = correlate(
        widened.reshape(3 * channels, length + 2 * reach), short_taps[:, ::-1]
    ).reshape(3, channels, -1)
    query_feat, key_feat, value_feat = (feats[0], feats[1], feats[2])
    product = key_feat * value_feat
    convolved = correlate(product, long_filter[:, ::-1])
    summed = convolved + skip_gain[:, None] * product[:, taps_long - 1 :]
    query_tail = query_feat[:, taps_long - 1 :]
    gated = (query_tail[:, :length] * summed[:, :length]).astype(jnp.bfloat16)

    gated_all = lax.all_gather(gated, "seq", axis=1, tiled=True)
    partial_out = lax.dot_general(
        out_weight, gated_all, (((0,), (0,)), ((), ())), preferred_element_type=jnp.float32
    )
    group = n_tp // n_seq
    out_rows = slab_width // group
    partial_out = (
        partial_out.reshape(group, out_rows, n_seq, length)
        .transpose(0, 2, 1, 3)
        .reshape(n_tp * out_rows, length)
    )
    output_sum = lax.psum_scatter(partial_out, "tp", scatter_dimension=0, tiled=True)
    route = []
    for s in range(n_seq):
        for p in range(n_tp):
            route.append((s * n_tp + p, (p % n_seq) * n_tp + group * s + p // n_seq))
    mixed = lax.ppermute(output_sum.astype(jnp.bfloat16), ("seq", "tp"), route)

    scale = 1.0 / math.sqrt(length * n_seq)
    terms = lax.dot_general(
        gated_all.reshape(channels, n_seq, length),
        slab_grad.reshape(slab_width, n_seq, length),
        (((2,), (2,)), ((1,), (1,))),
        preferred_element_type=jnp.float32,
    )
    terms = lax.reduce_precision(terms * scale, exponent_bits=8, mantissa_bits=7)
    weight_grad = jnp.sum(terms, axis=0).astype(jnp.bfloat16)

    next_grad = from_behind(gated_grad[:, :reach].astype(jnp.bfloat16), "seq", -1).astype(
        jnp.float32
    )
    grad_ext = jnp.concatenate([gated_grad, next_grad], axis=1)
    conv_grad = grad_ext * query_tail
    keep = length + taps_short - 1
    prod_grad = correlate(conv_grad, long_filter) + skip_gain[:, None] * conv_grad[:, :keep]
    query_grad = grad_ext[:, :keep] * summed[:, :keep]
    key_grad = prod_grad * value_feat[:, taps_long - 1 : taps_long - 1 + keep]
    value_grad = prod_grad * key_feat[:, taps_long - 1 : taps_long - 1 + keep]
    feat_grad = jnp.stack([query_grad, key_grad, value_grad]).reshape(3 * channels, keep)
    stream_grad = correlate(feat_grad, short_taps).reshape(3, channels, length).astype(jnp.bfloat16)
    return (mixed, stream_grad, weight_grad)


def solution(mesh):
    return jax.shard_map(
        shards,
        mesh=mesh,
        in_specs=(
            P(None, "tp", "seq"),
            P(None, "tp", None),
            P("tp", None),
            P("tp"),
            P("tp", "seq"),
            P("tp", "seq"),
        ),
        out_specs=(P("tp", "seq"), P(None, "tp", "seq"), P("tp", "seq")),
        check_vma=False,
    )
```

```python
import math

import jax
import jax.numpy as jnp
from jax import lax
from jax.sharding import PartitionSpec as P


def extended(block, axis, width):
    count = lax.axis_size(axis)
    forward = [(i, i + 1) for i in range(count - 1)]
    backward = [(target, source) for source, target in forward]
    low = lax.ppermute(block[..., block.shape[-1] - width :], axis, forward)
    high = lax.ppermute(block[..., :width], axis, backward)
    return jnp.concatenate([low, block, high], axis=-1)


def from_behind(block, axis, distance):
    devices = range(lax.axis_size(axis))
    route = [(i - distance, i) for i in devices if i - distance in devices]
    return lax.ppermute(block, axis, route)


def correlate(signal, taps):
    return lax.conv_general_dilated(
        signal[None],
        taps[:, None, :],
        (1,),
        "VALID",
        dimension_numbers=("NCH", "OIH", "NCH"),
        feature_group_count=signal.shape[0],
        precision=lax.Precision.HIGHEST,
    )[0]


def short_correlate(signal, taps):
    span = signal.shape[-1] - taps.shape[-1] + 1
    total = taps[..., 0:1] * signal[..., 0:span]
    for k in range(1, taps.shape[-1]):
        total = total + taps[..., k : k + 1] * signal[..., k : k + span]
    return total


def partner(index, step, count):
    if count & (count - 1) == 0:
        return index ^ step
    return (index + step) % count


def exchange(block_of, axis):
    count = lax.axis_size(axis)
    got = []
    for step in range(1, count):
        route = [(i, partner(i, step, count)) for i in range(count)]
        got.append(lax.ppermute(block_of(step), axis, route))
    return got


def rows_of_slab(out_grad, n_seq, n_tp):
    rows, length = out_grad.shape
    piece = rows // n_seq
    mine = lax.all_to_all(out_grad.reshape(n_seq, piece, length), "seq", 0, 0)
    mine = jnp.transpose(mine, (1, 0, 2)).reshape(piece, n_seq * length)
    route = []
    for a in range(n_seq):
        for b in range(n_tp):
            flat = n_seq * b + a
            route.append((a * n_tp + b, (flat // n_tp) * n_tp + flat % n_tp))
    moved = lax.ppermute(mine, ("seq", "tp"), route)
    return lax.all_gather(moved, "tp", axis=0, tiled=True)


def shards(streams, feat_weight, long_filter, skip_gain, out_weight, out_grad):
    channels = streams.shape[1]
    length = streams.shape[2]
    taps_long = long_filter.shape[1]
    taps_short = feat_weight.shape[2]
    n_seq = lax.axis_size("seq")
    n_tp = lax.axis_size("tp")
    me = lax.axis_index("seq")
    reach = taps_long + taps_short - 2
    keep = length + taps_short - 1

    slab_grad = rows_of_slab(out_grad, n_seq, n_tp)
    slab_width = slab_grad.shape[0]
    partial_grad = jnp.dot(out_weight, slab_grad, preferred_element_type=jnp.float32)

    def grad_block(step):
        start = partner(me, step, n_seq) * length
        return lax.dynamic_slice_in_dim(partial_grad, start, length, axis=1)

    arrived = exchange(grad_block, "seq")
    gated_grad = lax.dynamic_slice_in_dim(partial_grad, me * length, length, axis=1)
    for block in arrived:
        gated_grad = gated_grad + block

    widened = extended(streams, "seq", reach).astype(jnp.float32)
    key_value = short_correlate(
        widened[1:, :, : taps_long - 1 + keep + taps_short - 1], feat_weight[1:, :, ::-1]
    )
    key_feat, value_feat = key_value[0], key_value[1]
    query_tail = short_correlate(widened[0, :, taps_long - 1 :], feat_weight[0, :, ::-1])
    product = key_feat * value_feat
    convolved = correlate(product, long_filter[:, ::-1])
    summed = convolved + skip_gain[:, None] * product[:, taps_long - 1 :]
    gated = (query_tail[:, :length] * summed[:, :length]).astype(jnp.bfloat16)

    gated_blocks = [gated] + exchange(lambda step: gated, "seq")
    group = n_tp // n_seq
    out_rows = slab_width // group
    pieces = []
    for j in range(group):
        rows = out_weight[:, j * out_rows : (j + 1) * out_rows]
        for block in gated_blocks:
            pieces.append(
                lax.dot_general(
                    rows, block, (((0,), (0,)), ((), ())), preferred_element_type=jnp.float32
                )
            )
    partial_out = jnp.concatenate(pieces, axis=0)
    output_sum = lax.psum_scatter(partial_out, "tp", scatter_dimension=0, tiled=True)
    route = []
    for s in range(n_seq):
        for p in range(n_tp):
            target = partner(s, p % n_seq, n_seq) if p % n_seq else s
            route.append((s * n_tp + p, target * n_tp + group * s + p // n_seq))
    mixed = lax.ppermute(output_sum.astype(jnp.bfloat16), ("seq", "tp"), route)

    scale = 1.0 / math.sqrt(length * n_seq)
    weight_sum = None
    for step, block in enumerate(gated_blocks):
        source = partner(me, step, n_seq) if step else me
        grad_part = lax.dynamic_slice_in_dim(slab_grad, source * length, length, axis=1)
        term = lax.dot_general(
            block, grad_part, (((1,), (1,)), ((), ())), preferred_element_type=jnp.float32
        )
        term = lax.reduce_precision(term * scale, exponent_bits=8, mantissa_bits=7)
        weight_sum = term if weight_sum is None else weight_sum + term
    weight_grad = weight_sum.astype(jnp.bfloat16)

    next_grad = from_behind(gated_grad[:, :reach].astype(jnp.bfloat16), "seq", -1).astype(
        jnp.float32
    )
    grad_ext = jnp.concatenate([gated_grad, next_grad], axis=1)
    conv_grad = grad_ext * query_tail
    prod_grad = correlate(conv_grad, long_filter) + skip_gain[:, None] * conv_grad[:, :keep]
    query_grad = grad_ext[:, :keep] * summed[:, :keep]
    key_grad = prod_grad * value_feat[:, taps_long - 1 : taps_long - 1 + keep]
    value_grad = prod_grad * key_feat[:, taps_long - 1 : taps_long - 1 + keep]
    feat_grad = jnp.stack([query_grad, key_grad, value_grad])
    stream_grad = short_correlate(feat_grad, feat_weight).astype(jnp.bfloat16)
    return (mixed, stream_grad, weight_grad)


def solution(mesh):
    return jax.shard_map(
        shards,
        mesh=mesh,
        in_specs=(
            P(None, "tp", "seq"),
            P(None, "tp", None),
            P("tp", None),
            P("tp"),
            P("tp", "seq"),
            P("tp", "seq"),
        ),
        out_specs=(P("tp", "seq"), P(None, "tp", "seq"), P("tp", "seq")),
        check_vma=False,
    )
```

```python
import math

import jax
import jax.numpy as jnp
from jax import lax
from jax.sharding import PartitionSpec as P


def extended(block, axis, width):
    count = lax.axis_size(axis)
    forward = [(i, i + 1) for i in range(count - 1)]
    backward = [(target, source) for source, target in forward]
    low = lax.ppermute(block[..., block.shape[-1] - width :], axis, forward)
    high = lax.ppermute(block[..., :width], axis, backward)
    return jnp.concatenate([low, block, high], axis=-1)


def from_behind(block, axis, distance):
    devices = range(lax.axis_size(axis))
    route = [(i - distance, i) for i in devices if i - distance in devices]
    return lax.ppermute(block, axis, route)


def correlate(signal, taps):
    return lax.conv_general_dilated(
        signal[None],
        taps[:, None, :],
        (1,),
        "VALID",
        dimension_numbers=("NCH", "OIH", "NCH"),
        feature_group_count=signal.shape[0],
        precision=lax.Precision.HIGHEST,
    )[0]


def short_correlate(signal, taps):
    span = signal.shape[-1] - taps.shape[-1] + 1
    total = taps[..., 0:1] * signal[..., 0:span]
    for k in range(1, taps.shape[-1]):
        total = total + taps[..., k : k + 1] * signal[..., k : k + span]
    return total


def partner(index, step, count):
    if count & (count - 1) == 0:
        return index ^ step
    return (index + step) % count


def source(index, step, count):
    if count & (count - 1) == 0:
        return index ^ step
    return (index - step) % count


def exchange(block_of, axis):
    count = lax.axis_size(axis)
    got = []
    for step in range(1, count):
        route = [(i, partner(i, step, count)) for i in range(count)]
        got.append(lax.ppermute(block_of(step), axis, route))
    return got


def rows_of_slab(out_grad, n_seq, n_tp):
    rows, length = out_grad.shape
    piece = rows // n_seq
    me = lax.axis_index("seq")
    split = out_grad.reshape(n_seq, piece, length)
    got = exchange(lambda step: split[partner(me, step, n_seq)], "seq")
    stacked = jnp.stack([split[me]] + got)
    index = jnp.zeros((n_seq,), jnp.int32)
    for step in range(1, n_seq):
        index = index + jnp.where(
            jnp.arange(n_seq) == source(me, step, n_seq), step, 0
        ).astype(jnp.int32)
    mine = jnp.take(stacked, index, axis=0)
    mine = jnp.transpose(mine, (1, 0, 2)).reshape(piece, n_seq * length)
    route = []
    for a in range(n_seq):
        for b in range(n_tp):
            flat = n_seq * b + a
            route.append((a * n_tp + b, (flat // n_tp) * n_tp + flat % n_tp))
    moved = lax.ppermute(mine, ("seq", "tp"), route)
    return lax.all_gather(moved, "tp", axis=0, tiled=True)


def shards(streams, feat_weight, long_filter, skip_gain, out_weight, out_grad):
    channels = streams.shape[1]
    length = streams.shape[2]
    taps_long = long_filter.shape[1]
    taps_short = feat_weight.shape[2]
    n_seq = lax.axis_size("seq")
    n_tp = lax.axis_size("tp")
    me = lax.axis_index("seq")
    reach = taps_long + taps_short - 2
    keep = length + taps_short - 1

    widened = extended(streams, "seq", reach).astype(jnp.float32)
    slab_grad = rows_of_slab(out_grad, n_seq, n_tp)
    slab_width = slab_grad.shape[0]

    key_value = short_correlate(
        widened[1:, :, : taps_long - 1 + keep + taps_short - 1], feat_weight[1:, :, ::-1]
    )
    key_feat, value_feat = key_value[0], key_value[1]
    query_tail = short_correlate(widened[0, :, taps_long - 1 :], feat_weight[0, :, ::-1])
    product = key_feat * value_feat
    convolved = correlate(product, long_filter[:, ::-1])
    summed = convolved + skip_gain[:, None] * product[:, taps_long - 1 :]
    gated = (query_tail[:, :length] * summed[:, :length]).astype(jnp.bfloat16)

    gated_blocks = [gated] + exchange(lambda step: gated, "seq")
    group = n_tp // n_seq
    out_rows = slab_width // group
    pieces = []
    for j in range(group):
        rows = out_weight[:, j * out_rows : (j + 1) * out_rows]
        for block in gated_blocks:
            pieces.append(
                lax.dot_general(
                    rows, block, (((0,), (0,)), ((), ())), preferred_element_type=jnp.float32
                )
            )
    partial_out = jnp.concatenate(pieces, axis=0)
    output_sum = lax.psum_scatter(partial_out, "tp", scatter_dimension=0, tiled=True)
    route = []
    for s in range(n_seq):
        for p in range(n_tp):
            target = source(s, p % n_seq, n_seq) if p % n_seq else s
            route.append((s * n_tp + p, target * n_tp + group * s + p // n_seq))
    mixed = lax.ppermute(output_sum.astype(jnp.bfloat16), ("seq", "tp"), route)

    slab_grad, gated_blocks = lax.optimization_barrier((slab_grad, gated_blocks))
    partial_grad = jnp.dot(out_weight, slab_grad, preferred_element_type=jnp.float32)

    def grad_block(step):
        start = partner(me, step, n_seq) * length
        block = lax.dynamic_slice_in_dim(partial_grad, start, length, axis=1)
        return block.astype(jnp.bfloat16)

    arrived = exchange(grad_block, "seq")
    gated_grad = lax.dynamic_slice_in_dim(partial_grad, me * length, length, axis=1)
    for block in arrived:
        gated_grad = gated_grad + block.astype(jnp.float32)

    scale = 1.0 / math.sqrt(length * n_seq)
    weight_sum = None
    for step, block in enumerate(gated_blocks):
        origin = source(me, step, n_seq) if step else me
        grad_part = lax.dynamic_slice_in_dim(slab_grad, origin * length, length, axis=1)
        term = lax.dot_general(
            block, grad_part, (((1,), (1,)), ((), ())), preferred_element_type=jnp.float32
        )
        term = lax.reduce_precision(term * scale, exponent_bits=8, mantissa_bits=7)
        weight_sum = term if weight_sum is None else weight_sum + term
    weight_grad = weight_sum.astype(jnp.bfloat16)

    next_grad = from_behind(gated_grad[:, :reach].astype(jnp.bfloat16), "seq", -1).astype(
        jnp.float32
    )
    grad_ext = jnp.concatenate([gated_grad, next_grad], axis=1)
    conv_grad = grad_ext * query_tail
    prod_grad = correlate(conv_grad, long_filter) + skip_gain[:, None] * conv_grad[:, :keep]
    query_grad = grad_ext[:, :keep] * summed[:, :keep]
    key_grad = prod_grad * value_feat[:, taps_long - 1 : taps_long - 1 + keep]
    value_grad = prod_grad * key_feat[:, taps_long - 1 : taps_long - 1 + keep]
    feat_grad = jnp.stack([query_grad, key_grad, value_grad])
    stream_grad = short_correlate(feat_grad, feat_weight).astype(jnp.bfloat16)
    return (mixed, stream_grad, weight_grad)


def solution(mesh):
    return jax.shard_map(
        shards,
        mesh=mesh,
        in_specs=(
            P(None, "tp", "seq"),
            P(None, "tp", None),
            P("tp", None),
            P("tp"),
            P("tp", "seq"),
            P("tp", "seq"),
        ),
        out_specs=(P("tp", "seq"), P(None, "tp", "seq"), P("tp", "seq")),
        check_vma=False,
    )
```

```python
import math

import jax
import jax.numpy as jnp
from jax import lax
from jax.sharding import PartitionSpec as P


def halo(block, axis, width, short):
    count = lax.axis_size(axis)
    forward = [(i, i + 1) for i in range(count - 1)]
    backward = [(target, source) for source, target in forward]
    length = block.shape[-1]
    low = jnp.concatenate(
        [block[1, :, length - width :], block[2, :, length - width :], block[0, :, length - short :]],
        axis=-1,
    )
    high = jnp.concatenate([block[0, :, :width], block[1, :, :short], block[2, :, :short]], axis=-1)
    low = lax.ppermute(low, axis, forward)
    high = lax.ppermute(high, axis, backward)
    query = jnp.concatenate([low[:, 2 * width :], block[0], high[:, :width]], axis=-1)
    key = jnp.concatenate([low[:, :width], block[1], high[:, width : width + short]], axis=-1)
    value = jnp.concatenate(
        [low[:, width : 2 * width], block[2], high[:, width + short :]], axis=-1
    )
    return query, jnp.stack([key, value])


def from_behind(block, axis, distance):
    devices = range(lax.axis_size(axis))
    route = [(i - distance, i) for i in devices if i - distance in devices]
    return lax.ppermute(block, axis, route)


def correlate(signal, taps):
    return lax.conv_general_dilated(
        signal[None],
        taps[:, None, :],
        (1,),
        "VALID",
        dimension_numbers=("NCH", "OIH", "NCH"),
        feature_group_count=signal.shape[0],
        precision=lax.Precision.HIGHEST,
    )[0]


def short_correlate(signal, taps):
    span = signal.shape[-1] - taps.shape[-1] + 1
    total = taps[..., 0:1] * signal[..., 0:span]
    for k in range(1, taps.shape[-1]):
        total = total + taps[..., k : k + 1] * signal[..., k : k + span]
    return total


def partner(index, step, count):
    if count & (count - 1) == 0:
        return index ^ step
    return (index + step) % count


def source(index, step, count):
    if count & (count - 1) == 0:
        return index ^ step
    return (index - step) % count


def exchange(block_of, axis):
    count = lax.axis_size(axis)
    got = []
    for step in range(1, count):
        route = [(i, partner(i, step, count)) for i in range(count)]
        got.append(lax.ppermute(block_of(step), axis, route))
    return got


def rows_of_slab(out_grad, n_seq, n_tp):
    rows, length = out_grad.shape
    piece = rows // n_seq
    me = lax.axis_index("seq")
    split = out_grad.reshape(n_seq, piece, length)
    got = exchange(lambda step: split[partner(me, step, n_seq)], "seq")
    stacked = jnp.stack([split[me]] + got)
    index = jnp.zeros((n_seq,), jnp.int32)
    for step in range(1, n_seq):
        index = index + jnp.where(
            jnp.arange(n_seq) == source(me, step, n_seq), step, 0
        ).astype(jnp.int32)
    mine = jnp.take(stacked, index, axis=0)
    mine = jnp.transpose(mine, (1, 0, 2)).reshape(piece, n_seq * length)
    route = []
    for a in range(n_seq):
        for b in range(n_tp):
            flat = n_seq * b + a
            route.append((a * n_tp + b, (flat // n_tp) * n_tp + flat % n_tp))
    moved = lax.ppermute(mine, ("seq", "tp"), route)
    return lax.all_gather(moved, "tp", axis=0, tiled=True)


def shards(streams, feat_weight, long_filter, skip_gain, out_weight, out_grad):
    channels = streams.shape[1]
    length = streams.shape[2]
    taps_long = long_filter.shape[1]
    taps_short = feat_weight.shape[2]
    n_seq = lax.axis_size("seq")
    n_tp = lax.axis_size("tp")
    me = lax.axis_index("seq")
    reach = taps_long + taps_short - 2
    keep = length + taps_short - 1

    query_in, key_value_in = halo(streams, "seq", reach, taps_short - 1)
    slab_grad = rows_of_slab(out_grad, n_seq, n_tp)
    slab_width = slab_grad.shape[0]

    key_value = short_correlate(key_value_in.astype(jnp.float32), feat_weight[1:, :, ::-1])
    key_feat, value_feat = key_value[0], key_value[1]
    query_tail = short_correlate(query_in.astype(jnp.float32), feat_weight[0, :, ::-1])
    product = key_feat * value_feat
    convolved = correlate(product, long_filter[:, ::-1])
    summed = convolved + skip_gain[:, None] * product[:, taps_long - 1 :]
    gated = (query_tail[:, :length] * summed[:, :length]).astype(jnp.bfloat16)

    gated_blocks = [gated] + exchange(lambda step: gated, "seq")
    group = n_tp // n_seq
    out_rows = slab_width // group
    pieces = []
    for j in range(group):
        rows = out_weight[:, j * out_rows : (j + 1) * out_rows]
        for block in gated_blocks:
            pieces.append(
                lax.dot_general(
                    rows, block, (((0,), (0,)), ((), ())), preferred_element_type=jnp.float32
                ).astype(jnp.bfloat16)
            )
    partial_out = jnp.concatenate(pieces, axis=0)
    output_sum = lax.psum_scatter(partial_out, "tp", scatter_dimension=0, tiled=True)
    route = []
    for s in range(n_seq):
        for p in range(n_tp):
            target = source(s, p % n_seq, n_seq) if p % n_seq else s
            route.append((s * n_tp + p, target * n_tp + group * s + p // n_seq))
    mixed = lax.ppermute(output_sum, ("seq", "tp"), route)

    slab_grad, gated_blocks = lax.optimization_barrier((slab_grad, gated_blocks))
    partial_grad = jnp.dot(out_weight, slab_grad, preferred_element_type=jnp.float32)

    def grad_block(step):
        start = partner(me, step, n_seq) * length
        block = lax.dynamic_slice_in_dim(partial_grad, start, length, axis=1)
        return block.astype(jnp.bfloat16)

    arrived = exchange(grad_block, "seq")
    gated_grad = lax.dynamic_slice_in_dim(partial_grad, me * length, length, axis=1)
    for block in arrived:
        gated_grad = gated_grad + block.astype(jnp.float32)

    scale = 1.0 / math.sqrt(length * n_seq)
    weight_sum = None
    for step, block in enumerate(gated_blocks):
        origin = source(me, step, n_seq) if step else me
        grad_part = lax.dynamic_slice_in_dim(slab_grad, origin * length, length, axis=1)
        term = lax.dot_general(
            block, grad_part, (((1,), (1,)), ((), ())), preferred_element_type=jnp.float32
        )
        term = lax.reduce_precision(term * scale, exponent_bits=8, mantissa_bits=7)
        weight_sum = term if weight_sum is None else weight_sum + term
    weight_grad = weight_sum.astype(jnp.bfloat16)

    next_grad = from_behind(gated_grad[:, :reach].astype(jnp.bfloat16), "seq", -1).astype(
        jnp.float32
    )
    grad_ext = jnp.concatenate([gated_grad, next_grad], axis=1)
    conv_grad = grad_ext * query_tail
    prod_grad = correlate(conv_grad, long_filter) + skip_gain[:, None] * conv_grad[:, :keep]
    query_grad = grad_ext[:, :keep] * summed[:, :keep]
    key_grad = prod_grad * value_feat[:, taps_long - 1 : taps_long - 1 + keep]
    value_grad = prod_grad * key_feat[:, taps_long - 1 : taps_long - 1 + keep]
    feat_grad = jnp.stack([query_grad, key_grad, value_grad])
    stream_grad = short_correlate(feat_grad, feat_weight).astype(jnp.bfloat16)
    return (mixed, stream_grad, weight_grad)


def solution(mesh):
    return jax.shard_map(
        shards,
        mesh=mesh,
        in_specs=(
            P(None, "tp", "seq"),
            P(None, "tp", None),
            P("tp", None),
            P("tp"),
            P("tp", "seq"),
            P("tp", "seq"),
        ),
        out_specs=(P("tp", "seq"), P(None, "tp", "seq"), P("tp", "seq")),
        check_vma=False,
    )
```

```python
import math

import jax
import jax.numpy as jnp
from jax import lax
from jax.sharding import PartitionSpec as P


def halo(block, axis, width, short):
    count = lax.axis_size(axis)
    forward = [(i, i + 1) for i in range(count - 1)]
    backward = [(target, source) for source, target in forward]
    length = block.shape[-1]
    low = jnp.concatenate(
        [block[1, :, length - width :], block[2, :, length - width :], block[0, :, length - short :]],
        axis=-1,
    )
    high = jnp.concatenate([block[0, :, :width], block[1, :, :short], block[2, :, :short]], axis=-1)
    low = lax.ppermute(low, axis, forward)
    high = lax.ppermute(high, axis, backward)
    query = jnp.concatenate([low[:, 2 * width :], block[0], high[:, :width]], axis=-1)
    key = jnp.concatenate([low[:, :width], block[1], high[:, width : width + short]], axis=-1)
    value = jnp.concatenate(
        [low[:, width : 2 * width], block[2], high[:, width + short :]], axis=-1
    )
    return query, jnp.stack([key, value])


def from_behind(block, axis, distance):
    devices = range(lax.axis_size(axis))
    route = [(i - distance, i) for i in devices if i - distance in devices]
    return lax.ppermute(block, axis, route)


def correlate(signal, taps):
    return lax.conv_general_dilated(
        signal[None],
        taps[:, None, :],
        (1,),
        "VALID",
        dimension_numbers=("NCH", "OIH", "NCH"),
        feature_group_count=signal.shape[0],
        precision=lax.Precision.HIGHEST,
    )[0]


def short_correlate(signal, taps):
    span = signal.shape[-1] - taps.shape[-1] + 1
    total = taps[..., 0:1] * signal[..., 0:span]
    for k in range(1, taps.shape[-1]):
        total = total + taps[..., k : k + 1] * signal[..., k : k + span]
    return total


def partner(index, step, count):
    if count & (count - 1) == 0:
        return index ^ step
    return (index + step) % count


def source(index, step, count):
    if count & (count - 1) == 0:
        return index ^ step
    return (index - step) % count


def exchange(block_of, axis):
    count = lax.axis_size(axis)
    got = []
    for step in range(1, count):
        route = [(i, partner(i, step, count)) for i in range(count)]
        got.append(lax.ppermute(block_of(step), axis, route))
    return got


def rows_of_slab(out_grad, n_seq, n_tp):
    rows, length = out_grad.shape
    piece = rows // n_seq
    me = lax.axis_index("seq")
    split = out_grad.reshape(n_seq, piece, length)
    got = exchange(lambda step: split[partner(me, step, n_seq)], "seq")
    stacked = jnp.stack([split[me]] + got)
    index = jnp.zeros((n_seq,), jnp.int32)
    for step in range(1, n_seq):
        index = index + jnp.where(
            jnp.arange(n_seq) == source(me, step, n_seq), step, 0
        ).astype(jnp.int32)
    mine = jnp.take(stacked, index, axis=0)
    mine = jnp.transpose(mine, (1, 0, 2)).reshape(piece, n_seq * length)
    route = []
    for a in range(n_seq):
        for b in range(n_tp):
            flat = n_seq * b + a
            route.append((a * n_tp + b, (flat // n_tp) * n_tp + flat % n_tp))
    moved = lax.ppermute(mine, ("seq", "tp"), route)
    return lax.all_gather(moved, "tp", axis=0, tiled=True)


def shards(streams, feat_weight, long_filter, skip_gain, out_weight, out_grad):
    channels = streams.shape[1]
    length = streams.shape[2]
    taps_long = long_filter.shape[1]
    taps_short = feat_weight.shape[2]
    n_seq = lax.axis_size("seq")
    n_tp = lax.axis_size("tp")
    me = lax.axis_index("seq")
    reach = taps_long + taps_short - 2
    keep = length + taps_short - 1

    query_in, key_value_in = halo(streams, "seq", reach, taps_short - 1)
    slab_grad = rows_of_slab(out_grad, n_seq, n_tp)
    slab_width = slab_grad.shape[0]

    key_value = short_correlate(key_value_in.astype(jnp.float32), feat_weight[1:, :, ::-1])
    key_feat, value_feat = key_value[0], key_value[1]
    query_tail = short_correlate(query_in.astype(jnp.float32), feat_weight[0, :, ::-1])
    product = key_feat * value_feat
    convolved = correlate(product, long_filter[:, ::-1])
    summed = convolved + skip_gain[:, None] * product[:, taps_long - 1 :]
    gated = (query_tail[:, :length] * summed[:, :length]).astype(jnp.bfloat16)

    gated_blocks = [gated] + exchange(lambda step: gated, "seq")
    group = n_tp // n_seq
    weight_t = out_weight.T
    pieces = [
        jnp.dot(weight_t, block, preferred_element_type=jnp.float32).astype(jnp.bfloat16)
        for block in gated_blocks
    ]
    partial_out = jnp.concatenate(pieces, axis=0)
    output_sum = lax.psum_scatter(partial_out, "tp", scatter_dimension=0, tiled=True)
    route = []
    for s in range(n_seq):
        for p in range(n_tp):
            step = p // group
            target = source(s, step, n_seq) if step else s
            route.append((s * n_tp + p, target * n_tp + group * s + p % group))
    mixed = lax.ppermute(output_sum, ("seq", "tp"), route)

    slab_grad, gated_blocks = lax.optimization_barrier((slab_grad, gated_blocks))
    partial_grad = jnp.dot(out_weight, slab_grad, preferred_element_type=jnp.float32)

    def grad_block(step):
        start = partner(me, step, n_seq) * length
        block = lax.dynamic_slice_in_dim(partial_grad, start, length, axis=1)
        return block.astype(jnp.bfloat16)

    arrived = exchange(grad_block, "seq")
    gated_grad = lax.dynamic_slice_in_dim(partial_grad, me * length, length, axis=1)
    for block in arrived:
        gated_grad = gated_grad + block.astype(jnp.float32)

    scale = 1.0 / math.sqrt(length * n_seq)
    weight_sum = None
    for step, block in enumerate(gated_blocks):
        origin = source(me, step, n_seq) if step else me
        grad_part = lax.dynamic_slice_in_dim(slab_grad, origin * length, length, axis=1)
        term = lax.dot_general(
            block, grad_part, (((1,), (1,)), ((), ())), preferred_element_type=jnp.float32
        )
        term = lax.reduce_precision(term * scale, exponent_bits=8, mantissa_bits=7)
        weight_sum = term if weight_sum is None else weight_sum + term
    weight_grad = weight_sum.astype(jnp.bfloat16)

    next_grad = from_behind(gated_grad[:, :reach].astype(jnp.bfloat16), "seq", -1).astype(
        jnp.float32
    )
    grad_ext = jnp.concatenate([gated_grad, next_grad], axis=1)
    conv_grad = grad_ext * query_tail
    prod_grad = correlate(conv_grad, long_filter) + skip_gain[:, None] * conv_grad[:, :keep]
    query_grad = grad_ext[:, :keep] * summed[:, :keep]
    key_grad = prod_grad * value_feat[:, taps_long - 1 : taps_long - 1 + keep]
    value_grad = prod_grad * key_feat[:, taps_long - 1 : taps_long - 1 + keep]
    feat_grad = jnp.stack([query_grad, key_grad, value_grad])
    stream_grad = short_correlate(feat_grad, feat_weight).astype(jnp.bfloat16)
    return (mixed, stream_grad, weight_grad)


def solution(mesh):
    return jax.shard_map(
        shards,
        mesh=mesh,
        in_specs=(
            P(None, "tp", "seq"),
            P(None, "tp", None),
            P("tp", None),
            P("tp"),
            P("tp", "seq"),
            P("tp", "seq"),
        ),
        out_specs=(P("tp", "seq"), P(None, "tp", "seq"), P("tp", "seq")),
        check_vma=False,
    )
```

```python
import math

import jax
import jax.numpy as jnp
from jax import lax
from jax.sharding import PartitionSpec as P


def halo(block, axis, width, short):
    count = lax.axis_size(axis)
    forward = [(i, i + 1) for i in range(count - 1)]
    backward = [(target, source) for source, target in forward]
    length = block.shape[-1]
    low = jnp.concatenate(
        [block[1, :, length - width :], block[2, :, length - width :], block[0, :, length - short :]],
        axis=-1,
    )
    high = jnp.concatenate([block[0, :, :width], block[1, :, :short], block[2, :, :short]], axis=-1)
    low = lax.ppermute(low, axis, forward)
    high = lax.ppermute(high, axis, backward)
    query = jnp.concatenate([low[:, 2 * width :], block[0], high[:, :width]], axis=-1)
    key = jnp.concatenate([low[:, :width], block[1], high[:, width : width + short]], axis=-1)
    value = jnp.concatenate(
        [low[:, width : 2 * width], block[2], high[:, width + short :]], axis=-1
    )
    return query, jnp.stack([key, value])


def from_behind(block, axis, distance):
    devices = range(lax.axis_size(axis))
    route = [(i - distance, i) for i in devices if i - distance in devices]
    return lax.ppermute(block, axis, route)


def correlate(signal, taps):
    return lax.conv_general_dilated(
        signal[None],
        taps[:, None, :],
        (1,),
        "VALID",
        dimension_numbers=("NCH", "OIH", "NCH"),
        feature_group_count=signal.shape[0],
        precision=lax.Precision.HIGHEST,
    )[0]


def short_correlate(signal, taps):
    span = signal.shape[-1] - taps.shape[-1] + 1
    total = taps[..., 0:1] * signal[..., 0:span]
    for k in range(1, taps.shape[-1]):
        total = total + taps[..., k : k + 1] * signal[..., k : k + span]
    return total


def partner(index, step, count):
    if count & (count - 1) == 0:
        return index ^ step
    return (index + step) % count


def source(index, step, count):
    if count & (count - 1) == 0:
        return index ^ step
    return (index - step) % count


def exchange(block_of, axis):
    count = lax.axis_size(axis)
    got = []
    for step in range(1, count):
        route = [(i, partner(i, step, count)) for i in range(count)]
        got.append(lax.ppermute(block_of(step), axis, route))
    return got


def rows_of_slab(out_grad, n_seq, n_tp):
    rows, length = out_grad.shape
    piece = rows // n_seq
    me = lax.axis_index("seq")
    split = out_grad.reshape(n_seq, piece, length)
    got = exchange(lambda step: split[partner(me, step, n_seq)], "seq")
    stacked = jnp.stack([split[me]] + got)
    index = jnp.zeros((n_seq,), jnp.int32)
    for step in range(1, n_seq):
        index = index + jnp.where(
            jnp.arange(n_seq) == source(me, step, n_seq), step, 0
        ).astype(jnp.int32)
    mine = jnp.take(stacked, index, axis=0)
    mine = jnp.transpose(mine, (1, 0, 2)).reshape(piece, n_seq * length)
    route = []
    for a in range(n_seq):
        for b in range(n_tp):
            flat = n_seq * b + a
            route.append((a * n_tp + b, (flat // n_tp) * n_tp + flat % n_tp))
    moved = lax.ppermute(mine, ("seq", "tp"), route)
    return lax.all_gather(moved, "tp", axis=0, tiled=True)


def halving_scatter(total, axis):
    count = lax.axis_size(axis)
    if count & (count - 1):
        return lax.psum_scatter(total, axis, scatter_dimension=0, tiled=True)
    bits = count.bit_length() - 1
    me = lax.axis_index(axis)
    rows = total.shape[0] // count
    total = total.reshape([2] * bits + [rows, total.shape[1]])
    for level in range(bits):
        mask = 1 << level
        at = bits - 1 - level
        mine = (me // mask) % 2
        keep = lax.dynamic_index_in_dim(total, mine, at, keepdims=False)
        send = lax.dynamic_index_in_dim(total, 1 - mine, at, keepdims=False)
        route = [(i, i ^ mask) for i in range(count)]
        total = keep + lax.ppermute(send.astype(jnp.bfloat16), axis, route).astype(jnp.float32)
    return total


def shards(streams, feat_weight, long_filter, skip_gain, out_weight, out_grad):
    channels = streams.shape[1]
    length = streams.shape[2]
    taps_long = long_filter.shape[1]
    taps_short = feat_weight.shape[2]
    n_seq = lax.axis_size("seq")
    n_tp = lax.axis_size("tp")
    me = lax.axis_index("seq")
    reach = taps_long + taps_short - 2
    keep = length + taps_short - 1

    query_in, key_value_in = halo(streams, "seq", reach, taps_short - 1)
    slab_grad = rows_of_slab(out_grad, n_seq, n_tp)
    slab_width = slab_grad.shape[0]

    key_value = short_correlate(key_value_in.astype(jnp.float32), feat_weight[1:, :, ::-1])
    key_feat, value_feat = key_value[0], key_value[1]
    query_tail = short_correlate(query_in.astype(jnp.float32), feat_weight[0, :, ::-1])
    product = key_feat * value_feat
    convolved = correlate(product, long_filter[:, ::-1])
    summed = convolved + skip_gain[:, None] * product[:, taps_long - 1 :]
    gated = (query_tail[:, :length] * summed[:, :length]).astype(jnp.bfloat16)

    gated_blocks = [gated] + exchange(lambda step: gated, "seq")
    group = n_tp // n_seq
    weight_t = out_weight.T
    pieces = [jnp.dot(weight_t, block, preferred_element_type=jnp.float32) for block in gated_blocks]
    partial_out = jnp.concatenate(pieces, axis=0)
    output_sum = halving_scatter(partial_out, "tp").astype(jnp.bfloat16)
    route = []
    for s in range(n_seq):
        for p in range(n_tp):
            step = p // group
            target = source(s, step, n_seq) if step else s
            route.append((s * n_tp + p, target * n_tp + group * s + p % group))
    mixed = lax.ppermute(output_sum, ("seq", "tp"), route)

    slab_grad, gated_blocks = lax.optimization_barrier((slab_grad, gated_blocks))
    partial_grad = jnp.dot(out_weight, slab_grad, preferred_element_type=jnp.float32)

    def grad_block(step):
        start = partner(me, step, n_seq) * length
        block = lax.dynamic_slice_in_dim(partial_grad, start, length, axis=1)
        return block.astype(jnp.bfloat16)

    arrived = exchange(grad_block, "seq")
    gated_grad = lax.dynamic_slice_in_dim(partial_grad, me * length, length, axis=1)
    for block in arrived:
        gated_grad = gated_grad + block.astype(jnp.float32)

    scale = 1.0 / math.sqrt(length * n_seq)
    weight_sum = None
    for step, block in enumerate(gated_blocks):
        origin = source(me, step, n_seq) if step else me
        grad_part = lax.dynamic_slice_in_dim(slab_grad, origin * length, length, axis=1)
        term = lax.dot_general(
            block, grad_part, (((1,), (1,)), ((), ())), preferred_element_type=jnp.float32
        )
        term = lax.reduce_precision(term * scale, exponent_bits=8, mantissa_bits=7)
        weight_sum = term if weight_sum is None else weight_sum + term
    weight_grad = weight_sum.astype(jnp.bfloat16)

    next_grad = from_behind(gated_grad[:, :reach].astype(jnp.bfloat16), "seq", -1).astype(
        jnp.float32
    )
    grad_ext = jnp.concatenate([gated_grad, next_grad], axis=1)
    conv_grad = grad_ext * query_tail
    prod_grad = correlate(conv_grad, long_filter) + skip_gain[:, None] * conv_grad[:, :keep]
    query_grad = grad_ext[:, :keep] * summed[:, :keep]
    key_grad = prod_grad * value_feat[:, taps_long - 1 : taps_long - 1 + keep]
    value_grad = prod_grad * key_feat[:, taps_long - 1 : taps_long - 1 + keep]
    feat_grad = jnp.stack([query_grad, key_grad, value_grad])
    stream_grad = short_correlate(feat_grad, feat_weight).astype(jnp.bfloat16)
    return (mixed, stream_grad, weight_grad)


def solution(mesh):
    return jax.shard_map(
        shards,
        mesh=mesh,
        in_specs=(
            P(None, "tp", "seq"),
            P(None, "tp", None),
            P("tp", None),
            P("tp"),
            P("tp", "seq"),
            P("tp", "seq"),
        ),
        out_specs=(P("tp", "seq"), P(None, "tp", "seq"), P("tp", "seq")),
        check_vma=False,
    )
```

```python
import math

import jax
import jax.numpy as jnp
from jax import lax
from jax.sharding import PartitionSpec as P


def halo(block, axis, width, short):
    count = lax.axis_size(axis)
    forward = [(i, i + 1) for i in range(count - 1)]
    backward = [(target, source) for source, target in forward]
    length = block.shape[-1]
    low = jnp.concatenate(
        [block[1, :, length - width :], block[2, :, length - width :], block[0, :, length - short :]],
        axis=-1,
    )
    high = jnp.concatenate([block[0, :, :width], block[1, :, :short], block[2, :, :short]], axis=-1)
    low = lax.ppermute(low, axis, forward)
    high = lax.ppermute(high, axis, backward)
    query = jnp.concatenate([low[:, 2 * width :], block[0], high[:, :width]], axis=-1)
    key = jnp.concatenate([low[:, :width], block[1], high[:, width : width + short]], axis=-1)
    value = jnp.concatenate(
        [low[:, width : 2 * width], block[2], high[:, width + short :]], axis=-1
    )
    return query, jnp.stack([key, value])


def from_behind(block, axis, distance):
    devices = range(lax.axis_size(axis))
    route = [(i - distance, i) for i in devices if i - distance in devices]
    return lax.ppermute(block, axis, route)


def correlate(signal, taps):
    return lax.conv_general_dilated(
        signal[None],
        taps[:, None, :],
        (1,),
        "VALID",
        dimension_numbers=("NCH", "OIH", "NCH"),
        feature_group_count=signal.shape[0],
        precision=lax.Precision.HIGHEST,
    )[0]


def short_correlate(signal, taps):
    span = signal.shape[-1] - taps.shape[-1] + 1
    total = taps[..., 0:1] * signal[..., 0:span]
    for k in range(1, taps.shape[-1]):
        total = total + taps[..., k : k + 1] * signal[..., k : k + span]
    return total


def partner(index, step, count):
    if count & (count - 1) == 0:
        return index ^ step
    return (index + step) % count


def source(index, step, count):
    if count & (count - 1) == 0:
        return index ^ step
    return (index - step) % count


def exchange(block_of, axis):
    count = lax.axis_size(axis)
    got = []
    for step in range(1, count):
        route = [(i, partner(i, step, count)) for i in range(count)]
        got.append(lax.ppermute(block_of(step), axis, route))
    return got


def rows_of_slab(out_grad, n_seq, n_tp):
    rows, length = out_grad.shape
    piece = rows // n_seq
    me = lax.axis_index("seq")
    split = out_grad.reshape(n_seq, piece, length)
    got = exchange(lambda step: split[partner(me, step, n_seq)], "seq")
    stacked = jnp.stack([split[me]] + got)
    index = jnp.zeros((n_seq,), jnp.int32)
    for step in range(1, n_seq):
        index = index + jnp.where(
            jnp.arange(n_seq) == source(me, step, n_seq), step, 0
        ).astype(jnp.int32)
    mine = jnp.take(stacked, index, axis=0)
    mine = jnp.transpose(mine, (1, 0, 2)).reshape(piece, n_seq * length)
    route = []
    for a in range(n_seq):
        for b in range(n_tp):
            flat = n_seq * b + a
            route.append((a * n_tp + b, (flat // n_tp) * n_tp + flat % n_tp))
    moved = lax.ppermute(mine, ("seq", "tp"), route)
    return lax.all_gather(moved, "tp", axis=0, tiled=True)


def shards(streams, feat_weight, long_filter, skip_gain, out_weight, out_grad):
    channels = streams.shape[1]
    length = streams.shape[2]
    taps_long = long_filter.shape[1]
    taps_short = feat_weight.shape[2]
    n_seq = lax.axis_size("seq")
    n_tp = lax.axis_size("tp")
    me = lax.axis_index("seq")
    reach = taps_long + taps_short - 2
    keep = length + taps_short - 1

    query_in, key_value_in = halo(streams, "seq", reach, taps_short - 1)
    slab_grad = rows_of_slab(out_grad, n_seq, n_tp)
    slab_width = slab_grad.shape[0]

    key_value = short_correlate(key_value_in.astype(jnp.float32), feat_weight[1:, :, ::-1])
    key_feat, value_feat = key_value[0], key_value[1]
    query_tail = short_correlate(query_in.astype(jnp.float32), feat_weight[0, :, ::-1])
    product = key_feat * value_feat
    convolved = correlate(product, long_filter[:, ::-1])
    summed = convolved + skip_gain[:, None] * product[:, taps_long - 1 :]
    gated = (query_tail[:, :length] * summed[:, :length]).astype(jnp.bfloat16)

    gated_blocks = [gated] + exchange(lambda step: gated, "seq")
    group = n_tp // n_seq
    out_rows = slab_width // group
    pieces = []
    for j in range(group):
        rows = out_weight[:, j * out_rows : (j + 1) * out_rows]
        for block in gated_blocks:
            pieces.append(
                lax.dot_general(
                    rows, block, (((0,), (0,)), ((), ())), preferred_element_type=jnp.float32
                ).astype(jnp.bfloat16)
            )
    partial_out = jnp.concatenate(pieces, axis=0)
    output_sum = lax.psum_scatter(partial_out, "tp", scatter_dimension=0, tiled=True)
    route = []
    for s in range(n_seq):
        for p in range(n_tp):
            target = source(s, p % n_seq, n_seq) if p % n_seq else s
            route.append((s * n_tp + p, target * n_tp + group * s + p // n_seq))
    mixed_route = route

    slab_grad, gated_blocks = lax.optimization_barrier((slab_grad, gated_blocks))
    partial_grad = jnp.dot(out_weight, slab_grad, preferred_element_type=jnp.float32)

    def grad_block(step):
        start = partner(me, step, n_seq) * length
        block = lax.dynamic_slice_in_dim(partial_grad, start, length, axis=1)
        return block.astype(jnp.bfloat16)

    arrived = exchange(grad_block, "seq")
    gated_grad = lax.dynamic_slice_in_dim(partial_grad, me * length, length, axis=1)
    for block in arrived:
        gated_grad = gated_grad + block.astype(jnp.float32)

    scale = 1.0 / math.sqrt(length * n_seq)
    weight_sum = None
    for step, block in enumerate(gated_blocks):
        origin = source(me, step, n_seq) if step else me
        grad_part = lax.dynamic_slice_in_dim(slab_grad, origin * length, length, axis=1)
        term = lax.dot_general(
            block, grad_part, (((1,), (1,)), ((), ())), preferred_element_type=jnp.float32
        )
        term = lax.reduce_precision(term * scale, exponent_bits=8, mantissa_bits=7)
        weight_sum = term if weight_sum is None else weight_sum + term
    weight_grad = weight_sum.astype(jnp.bfloat16)

    next_grad = from_behind(gated_grad[:, :reach].astype(jnp.bfloat16), "seq", -1).astype(
        jnp.float32
    )
    grad_ext = jnp.concatenate([gated_grad, next_grad], axis=1)
    conv_grad = grad_ext * query_tail
    prod_grad = correlate(conv_grad, long_filter) + skip_gain[:, None] * conv_grad[:, :keep]
    query_grad = grad_ext[:, :keep] * summed[:, :keep]
    key_grad = prod_grad * value_feat[:, taps_long - 1 : taps_long - 1 + keep]
    value_grad = prod_grad * key_feat[:, taps_long - 1 : taps_long - 1 + keep]
    feat_grad = jnp.stack([query_grad, key_grad, value_grad])
    stream_grad = short_correlate(feat_grad, feat_weight).astype(jnp.bfloat16)
    output_sum, stream_grad, weight_grad = lax.optimization_barrier(
        (output_sum, stream_grad, weight_grad)
    )
    mixed = lax.ppermute(output_sum, ("seq", "tp"), mixed_route)
    return (mixed, stream_grad, weight_grad)


def solution(mesh):
    return jax.shard_map(
        shards,
        mesh=mesh,
        in_specs=(
            P(None, "tp", "seq"),
            P(None, "tp", None),
            P("tp", None),
            P("tp"),
            P("tp", "seq"),
            P("tp", "seq"),
        ),
        out_specs=(P("tp", "seq"), P(None, "tp", "seq"), P("tp", "seq")),
        check_vma=False,
    )
```

```python
import math

import jax
import jax.numpy as jnp
from jax import lax
from jax.sharding import PartitionSpec as P


def halo(block, axis, width, short):
    count = lax.axis_size(axis)
    forward = [(i, i + 1) for i in range(count - 1)]
    backward = [(target, source) for source, target in forward]
    length = block.shape[-1]
    low = jnp.concatenate(
        [block[1, :, length - width :], block[2, :, length - width :], block[0, :, length - short :]],
        axis=-1,
    )
    high = jnp.concatenate([block[0, :, :width], block[1, :, :short], block[2, :, :short]], axis=-1)
    low = lax.ppermute(low, axis, forward)
    high = lax.ppermute(high, axis, backward)
    query = jnp.concatenate([low[:, 2 * width :], block[0], high[:, :width]], axis=-1)
    key = jnp.concatenate([low[:, :width], block[1], high[:, width : width + short]], axis=-1)
    value = jnp.concatenate(
        [low[:, width : 2 * width], block[2], high[:, width + short :]], axis=-1
    )
    return query, jnp.stack([key, value])


def from_behind(block, axis, distance):
    devices = range(lax.axis_size(axis))
    route = [(i - distance, i) for i in devices if i - distance in devices]
    return lax.ppermute(block, axis, route)


def correlate(signal, taps):
    return lax.conv_general_dilated(
        signal[None],
        taps[:, None, :],
        (1,),
        "VALID",
        dimension_numbers=("NCH", "OIH", "NCH"),
        feature_group_count=signal.shape[0],
        precision=lax.Precision.HIGHEST,
    )[0]


def short_correlate(signal, taps):
    span = signal.shape[-1] - taps.shape[-1] + 1
    total = taps[..., 0:1] * signal[..., 0:span]
    for k in range(1, taps.shape[-1]):
        total = total + taps[..., k : k + 1] * signal[..., k : k + span]
    return total


def partner(index, step, count):
    if count & (count - 1) == 0:
        return index ^ step
    return (index + step) % count


def source(index, step, count):
    if count & (count - 1) == 0:
        return index ^ step
    return (index - step) % count


def exchange(block_of, axis):
    count = lax.axis_size(axis)
    got = []
    for step in range(1, count):
        route = [(i, partner(i, step, count)) for i in range(count)]
        got.append(lax.ppermute(block_of(step), axis, route))
    return got


def rows_of_slab(out_grad, n_seq, n_tp):
    rows, length = out_grad.shape
    piece = rows // n_seq
    me = lax.axis_index("seq")
    split = out_grad.reshape(n_seq, piece, length)
    got = exchange(lambda step: split[partner(me, step, n_seq)], "seq")
    stacked = jnp.stack([split[me]] + got)
    index = jnp.zeros((n_seq,), jnp.int32)
    for step in range(1, n_seq):
        index = index + jnp.where(
            jnp.arange(n_seq) == source(me, step, n_seq), step, 0
        ).astype(jnp.int32)
    mine = jnp.take(stacked, index, axis=0)
    mine = jnp.transpose(mine, (1, 0, 2)).reshape(piece, n_seq * length)
    route = []
    for a in range(n_seq):
        for b in range(n_tp):
            flat = n_seq * b + a
            route.append((a * n_tp + b, (flat // n_tp) * n_tp + flat % n_tp))
    moved = lax.ppermute(mine, ("seq", "tp"), route)
    return lax.all_gather(moved, "tp", axis=0, tiled=True)


def shards(streams, feat_weight, long_filter, skip_gain, out_weight, out_grad):
    channels = streams.shape[1]
    length = streams.shape[2]
    taps_long = long_filter.shape[1]
    taps_short = feat_weight.shape[2]
    n_seq = lax.axis_size("seq")
    n_tp = lax.axis_size("tp")
    me = lax.axis_index("seq")
    reach = taps_long + taps_short - 2
    keep = length + taps_short - 1

    query_in, key_value_in = halo(streams, "seq", reach, taps_short - 1)
    slab_grad = rows_of_slab(out_grad, n_seq, n_tp)
    slab_width = slab_grad.shape[0]

    key_value = short_correlate(key_value_in.astype(jnp.float32), feat_weight[1:, :, ::-1])
    key_feat, value_feat = key_value[0], key_value[1]
    query_tail = short_correlate(query_in.astype(jnp.float32), feat_weight[0, :, ::-1])
    product = key_feat * value_feat
    convolved = correlate(product, long_filter[:, ::-1])
    summed = convolved + skip_gain[:, None] * product[:, taps_long - 1 :]
    gated = (query_tail[:, :length] * summed[:, :length]).astype(jnp.bfloat16)

    gated_blocks = [gated] + exchange(lambda step: gated, "seq")
    group = n_tp // n_seq
    weight_t = out_weight.T
    pieces = [
        jnp.dot(weight_t, block, preferred_element_type=jnp.float32).astype(jnp.bfloat16)
        for block in gated_blocks
    ]
    partial_out = jnp.concatenate(pieces, axis=0)
    output_sum = lax.psum_scatter(partial_out, "tp", scatter_dimension=0, tiled=True)
    route = []
    for s in range(n_seq):
        for p in range(n_tp):
            step = p // group
            target = source(s, step, n_seq) if step else s
            route.append((s * n_tp + p, target * n_tp + group * s + p % group))
    mixed_route = route

    slab_grad, gated_blocks = lax.optimization_barrier((slab_grad, gated_blocks))
    partial_grad = jnp.dot(out_weight, slab_grad, preferred_element_type=jnp.float32)

    def grad_block(step):
        start = partner(me, step, n_seq) * length
        block = lax.dynamic_slice_in_dim(partial_grad, start, length, axis=1)
        return block.astype(jnp.bfloat16)

    arrived = exchange(grad_block, "seq")
    gated_grad = lax.dynamic_slice_in_dim(partial_grad, me * length, length, axis=1)
    for block in arrived:
        gated_grad = gated_grad + block.astype(jnp.float32)

    scale = 1.0 / math.sqrt(length * n_seq)
    weight_sum = None
    for step, block in enumerate(gated_blocks):
        origin = source(me, step, n_seq) if step else me
        grad_part = lax.dynamic_slice_in_dim(slab_grad, origin * length, length, axis=1)
        term = lax.dot_general(
            block, grad_part, (((1,), (1,)), ((), ())), preferred_element_type=jnp.float32
        )
        term = lax.reduce_precision(term * scale, exponent_bits=8, mantissa_bits=7)
        weight_sum = term if weight_sum is None else weight_sum + term
    weight_grad = weight_sum.astype(jnp.bfloat16)

    next_grad = from_behind(gated_grad[:, :reach].astype(jnp.bfloat16), "seq", -1).astype(
        jnp.float32
    )
    grad_ext = jnp.concatenate([gated_grad, next_grad], axis=1)
    conv_grad = grad_ext * query_tail
    prod_grad = correlate(conv_grad, long_filter) + skip_gain[:, None] * conv_grad[:, :keep]
    query_grad = grad_ext[:, :keep] * summed[:, :keep]
    key_grad = prod_grad * value_feat[:, taps_long - 1 : taps_long - 1 + keep]
    value_grad = prod_grad * key_feat[:, taps_long - 1 : taps_long - 1 + keep]
    feat_grad = jnp.stack([query_grad, key_grad, value_grad])
    stream_grad = short_correlate(feat_grad, feat_weight).astype(jnp.bfloat16)
    output_sum, stream_grad, weight_grad = lax.optimization_barrier(
        (output_sum, stream_grad, weight_grad)
    )
    mixed = lax.ppermute(output_sum, ("seq", "tp"), mixed_route)
    return (mixed, stream_grad, weight_grad)


def solution(mesh):
    return jax.shard_map(
        shards,
        mesh=mesh,
        in_specs=(
            P(None, "tp", "seq"),
            P(None, "tp", None),
            P("tp", None),
            P("tp"),
            P("tp", "seq"),
            P("tp", "seq"),
        ),
        out_specs=(P("tp", "seq"), P(None, "tp", "seq"), P("tp", "seq")),
        check_vma=False,
    )
```

```python
import math

import jax
import jax.numpy as jnp
from jax import lax
from jax.sharding import PartitionSpec as P


def halo(block, axis, width, short):
    count = lax.axis_size(axis)
    forward = [(i, i + 1) for i in range(count - 1)]
    backward = [(target, source) for source, target in forward]
    length = block.shape[-1]
    low = jnp.concatenate(
        [block[1, :, length - width :], block[2, :, length - width :], block[0, :, length - short :]],
        axis=-1,
    )
    high = jnp.concatenate([block[0, :, :width], block[1, :, :short], block[2, :, :short]], axis=-1)
    low = lax.ppermute(low, axis, forward)
    high = lax.ppermute(high, axis, backward)
    query = jnp.concatenate([low[:, 2 * width :], block[0], high[:, :width]], axis=-1)
    key = jnp.concatenate([low[:, :width], block[1], high[:, width : width + short]], axis=-1)
    value = jnp.concatenate(
        [low[:, width : 2 * width], block[2], high[:, width + short :]], axis=-1
    )
    return query, jnp.stack([key, value])


def from_behind(block, axis, distance):
    devices = range(lax.axis_size(axis))
    route = [(i - distance, i) for i in devices if i - distance in devices]
    return lax.ppermute(block, axis, route)


def correlate(signal, taps):
    return lax.conv_general_dilated(
        signal[None],
        taps[:, None, :],
        (1,),
        "VALID",
        dimension_numbers=("NCH", "OIH", "NCH"),
        feature_group_count=signal.shape[0],
        precision=lax.Precision.HIGHEST,
    )[0]


def short_correlate(signal, taps):
    span = signal.shape[-1] - taps.shape[-1] + 1
    total = taps[..., 0:1] * signal[..., 0:span]
    for k in range(1, taps.shape[-1]):
        total = total + taps[..., k : k + 1] * signal[..., k : k + span]
    return total


def partner(index, step, count):
    if count & (count - 1) == 0:
        return index ^ step
    return (index + step) % count


def source(index, step, count):
    if count & (count - 1) == 0:
        return index ^ step
    return (index - step) % count


def exchange(block_of, axis):
    count = lax.axis_size(axis)
    got = []
    for step in range(1, count):
        route = [(i, partner(i, step, count)) for i in range(count)]
        got.append(lax.ppermute(block_of(step), axis, route))
    return got


def rows_of_slab(out_grad, n_seq, n_tp):
    rows, length = out_grad.shape
    piece = rows // n_seq
    me = lax.axis_index("seq")
    split = out_grad.reshape(n_seq, piece, length)
    got = exchange(lambda step: split[partner(me, step, n_seq)], "seq")
    stacked = jnp.stack([split[me]] + got)
    index = jnp.zeros((n_seq,), jnp.int32)
    for step in range(1, n_seq):
        index = index + jnp.where(
            jnp.arange(n_seq) == source(me, step, n_seq), step, 0
        ).astype(jnp.int32)
    mine = jnp.take(stacked, index, axis=0)
    return jnp.transpose(mine, (1, 0, 2)).reshape(piece, n_seq * length)


def rows_gathered(mine, n_seq, n_tp):
    route = []
    for a in range(n_seq):
        for b in range(n_tp):
            flat = n_seq * b + a
            route.append((a * n_tp + b, (flat // n_tp) * n_tp + flat % n_tp))
    moved = lax.ppermute(mine, ("seq", "tp"), route)
    return lax.all_gather(moved, "tp", axis=0, tiled=True)


def shards(streams, feat_weight, long_filter, skip_gain, out_weight, out_grad):
    channels = streams.shape[1]
    length = streams.shape[2]
    taps_long = long_filter.shape[1]
    taps_short = feat_weight.shape[2]
    n_seq = lax.axis_size("seq")
    n_tp = lax.axis_size("tp")
    me = lax.axis_index("seq")
    reach = taps_long + taps_short - 2
    keep = length + taps_short - 1

    slab_piece = rows_of_slab(out_grad, n_seq, n_tp)
    streams, slab_piece = lax.optimization_barrier((streams, slab_piece))
    query_in, key_value_in = halo(streams, "seq", reach, taps_short - 1)
    slab_grad = rows_gathered(slab_piece, n_seq, n_tp)
    slab_width = slab_grad.shape[0]

    key_value = short_correlate(key_value_in.astype(jnp.float32), feat_weight[1:, :, ::-1])
    key_feat, value_feat = key_value[0], key_value[1]
    query_tail = short_correlate(query_in.astype(jnp.float32), feat_weight[0, :, ::-1])
    product = key_feat * value_feat
    convolved = correlate(product, long_filter[:, ::-1])
    summed = convolved + skip_gain[:, None] * product[:, taps_long - 1 :]
    gated = (query_tail[:, :length] * summed[:, :length]).astype(jnp.bfloat16)

    gated_blocks = [gated] + exchange(lambda step: gated, "seq")
    group = n_tp // n_seq
    weight_t = out_weight.T
    pieces = [
        jnp.dot(weight_t, block, preferred_element_type=jnp.float32).astype(jnp.bfloat16)
        for block in gated_blocks
    ]
    partial_out = jnp.concatenate(pieces, axis=0)
    output_sum = lax.psum_scatter(partial_out, "tp", scatter_dimension=0, tiled=True)
    route = []
    for s in range(n_seq):
        for p in range(n_tp):
            step = p // group
            target = source(s, step, n_seq) if step else s
            route.append((s * n_tp + p, target * n_tp + group * s + p % group))
    mixed_route = route

    slab_grad, gated_blocks = lax.optimization_barrier((slab_grad, gated_blocks))
    partial_grad = jnp.dot(out_weight, slab_grad, preferred_element_type=jnp.float32)

    def grad_block(step):
        start = partner(me, step, n_seq) * length
        block = lax.dynamic_slice_in_dim(partial_grad, start, length, axis=1)
        return block.astype(jnp.bfloat16)

    arrived = exchange(grad_block, "seq")
    gated_grad = lax.dynamic_slice_in_dim(partial_grad, me * length, length, axis=1)
    for block in arrived:
        gated_grad = gated_grad + block.astype(jnp.float32)

    scale = 1.0 / math.sqrt(length * n_seq)
    weight_sum = None
    for step, block in enumerate(gated_blocks):
        origin = source(me, step, n_seq) if step else me
        grad_part = lax.dynamic_slice_in_dim(slab_grad, origin * length, length, axis=1)
        term = lax.dot_general(
            block, grad_part, (((1,), (1,)), ((), ())), preferred_element_type=jnp.float32
        )
        term = lax.reduce_precision(term * scale, exponent_bits=8, mantissa_bits=7)
        weight_sum = term if weight_sum is None else weight_sum + term
    weight_grad = weight_sum.astype(jnp.bfloat16)

    next_grad = from_behind(gated_grad[:, :reach].astype(jnp.bfloat16), "seq", -1).astype(
        jnp.float32
    )
    grad_ext = jnp.concatenate([gated_grad, next_grad], axis=1)
    conv_grad = grad_ext * query_tail
    prod_grad = correlate(conv_grad, long_filter) + skip_gain[:, None] * conv_grad[:, :keep]
    query_grad = grad_ext[:, :keep] * summed[:, :keep]
    key_grad = prod_grad * value_feat[:, taps_long - 1 : taps_long - 1 + keep]
    value_grad = prod_grad * key_feat[:, taps_long - 1 : taps_long - 1 + keep]
    feat_grad = jnp.stack([query_grad, key_grad, value_grad])
    stream_grad = short_correlate(feat_grad, feat_weight).astype(jnp.bfloat16)
    output_sum, stream_grad, weight_grad = lax.optimization_barrier(
        (output_sum, stream_grad, weight_grad)
    )
    mixed = lax.ppermute(output_sum, ("seq", "tp"), mixed_route)
    return (mixed, stream_grad, weight_grad)


def solution(mesh):
    return jax.shard_map(
        shards,
        mesh=mesh,
        in_specs=(
            P(None, "tp", "seq"),
            P(None, "tp", None),
            P("tp", None),
            P("tp"),
            P("tp", "seq"),
            P("tp", "seq"),
        ),
        out_specs=(P("tp", "seq"), P(None, "tp", "seq"), P("tp", "seq")),
        check_vma=False,
    )
```

```python
import math

import jax
import jax.numpy as jnp
from jax import lax
from jax.sharding import PartitionSpec as P


def halo(block, axis, width, short):
    count = lax.axis_size(axis)
    forward = [(i, i + 1) for i in range(count - 1)]
    backward = [(target, source) for source, target in forward]
    length = block.shape[-1]
    low = jnp.concatenate(
        [block[1, :, length - width :], block[2, :, length - width :], block[0, :, length - short :]],
        axis=-1,
    )
    high = jnp.concatenate([block[0, :, :width], block[1, :, :short], block[2, :, :short]], axis=-1)
    low = lax.ppermute(low, axis, forward)
    high = lax.ppermute(high, axis, backward)
    query = jnp.concatenate([low[:, 2 * width :], block[0], high[:, :width]], axis=-1)
    key = jnp.concatenate([low[:, :width], block[1], high[:, width : width + short]], axis=-1)
    value = jnp.concatenate(
        [low[:, width : 2 * width], block[2], high[:, width + short :]], axis=-1
    )
    return query, jnp.stack([key, value])


def from_behind(block, axis, distance):
    devices = range(lax.axis_size(axis))
    route = [(i - distance, i) for i in devices if i - distance in devices]
    return lax.ppermute(block, axis, route)


def correlate(signal, taps):
    return lax.conv_general_dilated(
        signal[None],
        taps[:, None, :],
        (1,),
        "VALID",
        dimension_numbers=("NCH", "OIH", "NCH"),
        feature_group_count=signal.shape[0],
        precision=lax.Precision.HIGHEST,
    )[0]


def short_correlate(signal, taps):
    span = signal.shape[-1] - taps.shape[-1] + 1
    total = taps[..., 0:1] * signal[..., 0:span]
    for k in range(1, taps.shape[-1]):
        total = total + taps[..., k : k + 1] * signal[..., k : k + span]
    return total


def partner(index, step, count):
    if count & (count - 1) == 0:
        return index ^ step
    return (index + step) % count


def source(index, step, count):
    if count & (count - 1) == 0:
        return index ^ step
    return (index - step) % count


def exchange(block_of, axis):
    count = lax.axis_size(axis)
    got = []
    for step in range(1, count):
        route = [(i, partner(i, step, count)) for i in range(count)]
        got.append(lax.ppermute(block_of(step), axis, route))
    return got


def rows_of_slab(out_grad, n_seq, n_tp):
    rows, length = out_grad.shape
    piece = rows // n_seq
    me = lax.axis_index("seq")
    split = out_grad.reshape(n_seq, piece, length)
    got = []
    for k in range(n_seq):
        route = []
        for r in range(n_seq):
            for b in range(n_tp):
                route.append((r * n_tp + b, n_seq * b + (r + k) % n_seq))
        got.append(lax.ppermute(split[(me + k) % n_seq], ("seq", "tp"), route))
    stacked = jnp.stack(got)
    flat = me * n_tp + lax.axis_index("tp")
    index = (flat % n_seq - jnp.arange(n_seq)) % n_seq
    mine = jnp.take(stacked, index, axis=0)
    return jnp.transpose(mine, (1, 0, 2)).reshape(piece, n_seq * length)


def rows_gathered(mine, n_seq, n_tp):
    return lax.all_gather(mine, "tp", axis=0, tiled=True)


def shards(streams, feat_weight, long_filter, skip_gain, out_weight, out_grad):
    channels = streams.shape[1]
    length = streams.shape[2]
    taps_long = long_filter.shape[1]
    taps_short = feat_weight.shape[2]
    n_seq = lax.axis_size("seq")
    n_tp = lax.axis_size("tp")
    me = lax.axis_index("seq")
    reach = taps_long + taps_short - 2
    keep = length + taps_short - 1

    slab_piece = rows_of_slab(out_grad, n_seq, n_tp)
    streams, slab_piece = lax.optimization_barrier((streams, slab_piece))
    query_in, key_value_in = halo(streams, "seq", reach, taps_short - 1)
    slab_grad = rows_gathered(slab_piece, n_seq, n_tp)
    slab_width = slab_grad.shape[0]

    key_value = short_correlate(key_value_in.astype(jnp.float32), feat_weight[1:, :, ::-1])
    key_feat, value_feat = key_value[0], key_value[1]
    query_tail = short_correlate(query_in.astype(jnp.float32), feat_weight[0, :, ::-1])
    product = key_feat * value_feat
    convolved = correlate(product, long_filter[:, ::-1])
    summed = convolved + skip_gain[:, None] * product[:, taps_long - 1 :]
    gated = (query_tail[:, :length] * summed[:, :length]).astype(jnp.bfloat16)

    gated_blocks = [gated] + exchange(lambda step: gated, "seq")
    group = n_tp // n_seq
    weight_t = out_weight.T
    pieces = [
        jnp.dot(weight_t, block, preferred_element_type=jnp.float32).astype(jnp.bfloat16)
        for block in gated_blocks
    ]
    partial_out = jnp.concatenate(pieces, axis=0)
    output_sum = lax.psum_scatter(partial_out, "tp", scatter_dimension=0, tiled=True)
    route = []
    for s in range(n_seq):
        for p in range(n_tp):
            step = p // group
            target = source(s, step, n_seq) if step else s
            route.append((s * n_tp + p, target * n_tp + group * s + p % group))
    mixed_route = route

    slab_grad, gated_blocks = lax.optimization_barrier((slab_grad, gated_blocks))
    partial_grad = jnp.dot(out_weight, slab_grad, preferred_element_type=jnp.float32)

    def grad_block(step):
        start = partner(me, step, n_seq) * length
        block = lax.dynamic_slice_in_dim(partial_grad, start, length, axis=1)
        return block.astype(jnp.bfloat16)

    arrived = exchange(grad_block, "seq")
    gated_grad = lax.dynamic_slice_in_dim(partial_grad, me * length, length, axis=1)
    for block in arrived:
        gated_grad = gated_grad + block.astype(jnp.float32)

    scale = 1.0 / math.sqrt(length * n_seq)
    weight_sum = None
    for step, block in enumerate(gated_blocks):
        origin = source(me, step, n_seq) if step else me
        grad_part = lax.dynamic_slice_in_dim(slab_grad, origin * length, length, axis=1)
        term = lax.dot_general(
            block, grad_part, (((1,), (1,)), ((), ())), preferred_element_type=jnp.float32
        )
        term = lax.reduce_precision(term * scale, exponent_bits=8, mantissa_bits=7)
        weight_sum = term if weight_sum is None else weight_sum + term
    weight_grad = weight_sum.astype(jnp.bfloat16)

    next_grad = from_behind(gated_grad[:, :reach].astype(jnp.bfloat16), "seq", -1).astype(
        jnp.float32
    )
    grad_ext = jnp.concatenate([gated_grad, next_grad], axis=1)
    conv_grad = grad_ext * query_tail
    prod_grad = correlate(conv_grad, long_filter) + skip_gain[:, None] * conv_grad[:, :keep]
    query_grad = grad_ext[:, :keep] * summed[:, :keep]
    key_grad = prod_grad * value_feat[:, taps_long - 1 : taps_long - 1 + keep]
    value_grad = prod_grad * key_feat[:, taps_long - 1 : taps_long - 1 + keep]
    feat_grad = jnp.stack([query_grad, key_grad, value_grad])
    stream_grad = short_correlate(feat_grad, feat_weight).astype(jnp.bfloat16)
    output_sum, stream_grad, weight_grad = lax.optimization_barrier(
        (output_sum, stream_grad, weight_grad)
    )
    mixed = lax.ppermute(output_sum, ("seq", "tp"), mixed_route)
    return (mixed, stream_grad, weight_grad)


def solution(mesh):
    return jax.shard_map(
        shards,
        mesh=mesh,
        in_specs=(
            P(None, "tp", "seq"),
            P(None, "tp", None),
            P("tp", None),
            P("tp"),
            P("tp", "seq"),
            P("tp", "seq"),
        ),
        out_specs=(P("tp", "seq"), P(None, "tp", "seq"), P("tp", "seq")),
        check_vma=False,
    )
```

```python
import math

import jax
import jax.numpy as jnp
from jax import lax
from jax.sharding import PartitionSpec as P


def halo(block, axis, width, short):
    count = lax.axis_size(axis)
    forward = [(i, i + 1) for i in range(count - 1)]
    backward = [(target, source) for source, target in forward]
    length = block.shape[-1]
    low = jnp.concatenate(
        [block[1, :, length - width :], block[2, :, length - width :], block[0, :, length - short :]],
        axis=-1,
    )
    high = jnp.concatenate([block[0, :, :width], block[1, :, :short], block[2, :, :short]], axis=-1)
    low = lax.ppermute(low, axis, forward)
    high = lax.ppermute(high, axis, backward)
    query_head = jnp.concatenate([low[:, 2 * width :], block[0]], axis=-1)
    key_value_head = jnp.stack(
        [
            jnp.concatenate([low[:, :width], block[1]], axis=-1),
            jnp.concatenate([low[:, width : 2 * width], block[2]], axis=-1),
        ]
    )
    query = jnp.concatenate([query_head, high[:, :width]], axis=-1)
    key = jnp.concatenate([key_value_head[0], high[:, width : width + short]], axis=-1)
    value = jnp.concatenate([key_value_head[1], high[:, width + short :]], axis=-1)
    return query_head, key_value_head, query, jnp.stack([key, value])


def from_behind(block, axis, distance):
    devices = range(lax.axis_size(axis))
    route = [(i - distance, i) for i in devices if i - distance in devices]
    return lax.ppermute(block, axis, route)


def correlate(signal, taps):
    return lax.conv_general_dilated(
        signal[None],
        taps[:, None, :],
        (1,),
        "VALID",
        dimension_numbers=("NCH", "OIH", "NCH"),
        feature_group_count=signal.shape[0],
        precision=lax.Precision.HIGHEST,
    )[0]


def short_correlate(signal, taps):
    span = signal.shape[-1] - taps.shape[-1] + 1
    total = taps[..., 0:1] * signal[..., 0:span]
    for k in range(1, taps.shape[-1]):
        total = total + taps[..., k : k + 1] * signal[..., k : k + span]
    return total


def partner(index, step, count):
    if count & (count - 1) == 0:
        return index ^ step
    return (index + step) % count


def source(index, step, count):
    if count & (count - 1) == 0:
        return index ^ step
    return (index - step) % count


def exchange(block_of, axis):
    count = lax.axis_size(axis)
    got = []
    for step in range(1, count):
        route = [(i, partner(i, step, count)) for i in range(count)]
        got.append(lax.ppermute(block_of(step), axis, route))
    return got


def rows_of_slab(out_grad, n_seq, n_tp):
    rows, length = out_grad.shape
    piece = rows // n_seq
    me = lax.axis_index("seq")
    split = out_grad.reshape(n_seq, piece, length)
    got = exchange(lambda step: split[partner(me, step, n_seq)], "seq")
    stacked = jnp.stack([split[me]] + got)
    index = jnp.zeros((n_seq,), jnp.int32)
    for step in range(1, n_seq):
        index = index + jnp.where(
            jnp.arange(n_seq) == source(me, step, n_seq), step, 0
        ).astype(jnp.int32)
    mine = jnp.take(stacked, index, axis=0)
    return jnp.transpose(mine, (1, 0, 2)).reshape(piece, n_seq * length)


def rows_gathered(mine, n_seq, n_tp):
    route = []
    for a in range(n_seq):
        for b in range(n_tp):
            flat = n_seq * b + a
            route.append((a * n_tp + b, (flat // n_tp) * n_tp + flat % n_tp))
    moved = lax.ppermute(mine, ("seq", "tp"), route)
    return lax.all_gather(moved, "tp", axis=0, tiled=True)


def shards(streams, feat_weight, long_filter, skip_gain, out_weight, out_grad):
    channels = streams.shape[1]
    length = streams.shape[2]
    taps_long = long_filter.shape[1]
    taps_short = feat_weight.shape[2]
    n_seq = lax.axis_size("seq")
    n_tp = lax.axis_size("tp")
    me = lax.axis_index("seq")
    reach = taps_long + taps_short - 2
    keep = length + taps_short - 1

    slab_piece = rows_of_slab(out_grad, n_seq, n_tp)
    streams, slab_piece = lax.optimization_barrier((streams, slab_piece))
    query_head_in, key_value_head_in, query_in, key_value_in = halo(
        streams, "seq", reach, taps_short - 1
    )
    slab_grad = rows_gathered(slab_piece, n_seq, n_tp)
    slab_width = slab_grad.shape[0]

    key_value_head = short_correlate(
        key_value_head_in.astype(jnp.float32), feat_weight[1:, :, ::-1]
    )
    query_head = short_correlate(query_head_in.astype(jnp.float32), feat_weight[0, :, ::-1])
    product_head = key_value_head[0] * key_value_head[1]
    summed_head = correlate(product_head, long_filter[:, ::-1]) + (
        skip_gain[:, None] * product_head[:, taps_long - 1 :]
    )
    gated = (query_head * summed_head).astype(jnp.bfloat16)

    gated_blocks = [gated] + exchange(lambda step: gated, "seq")
    group = n_tp // n_seq
    weight_t = out_weight.T
    pieces = [
        jnp.dot(weight_t, block, preferred_element_type=jnp.float32).astype(jnp.bfloat16)
        for block in gated_blocks
    ]
    partial_out = jnp.concatenate(pieces, axis=0)
    output_sum = lax.psum_scatter(partial_out, "tp", scatter_dimension=0, tiled=True)
    route = []
    for s in range(n_seq):
        for p in range(n_tp):
            step = p // group
            target = source(s, step, n_seq) if step else s
            route.append((s * n_tp + p, target * n_tp + group * s + p % group))
    mixed_route = route

    key_value = short_correlate(key_value_in.astype(jnp.float32), feat_weight[1:, :, ::-1])
    key_feat, value_feat = key_value[0], key_value[1]
    query_tail = short_correlate(query_in.astype(jnp.float32), feat_weight[0, :, ::-1])
    product = key_feat * value_feat
    past = product[:, length:]
    summed_next = correlate(past, long_filter[:, ::-1]) + (
        skip_gain[:, None] * past[:, taps_long - 1 :]
    )
    summed = jnp.concatenate([summed_head, summed_next], axis=1)

    slab_grad, gated_blocks = lax.optimization_barrier((slab_grad, gated_blocks))
    partial_grad = jnp.dot(out_weight, slab_grad, preferred_element_type=jnp.float32)

    def grad_block(step):
        start = partner(me, step, n_seq) * length
        block = lax.dynamic_slice_in_dim(partial_grad, start, length, axis=1)
        return block.astype(jnp.bfloat16)

    arrived = exchange(grad_block, "seq")
    gated_grad = lax.dynamic_slice_in_dim(partial_grad, me * length, length, axis=1)
    for block in arrived:
        gated_grad = gated_grad + block.astype(jnp.float32)

    scale = 1.0 / math.sqrt(length * n_seq)
    weight_sum = None
    for step, block in enumerate(gated_blocks):
        origin = source(me, step, n_seq) if step else me
        grad_part = lax.dynamic_slice_in_dim(slab_grad, origin * length, length, axis=1)
        term = lax.dot_general(
            block, grad_part, (((1,), (1,)), ((), ())), preferred_element_type=jnp.float32
        )
        term = lax.reduce_precision(term * scale, exponent_bits=8, mantissa_bits=7)
        weight_sum = term if weight_sum is None else weight_sum + term
    weight_grad = weight_sum.astype(jnp.bfloat16)

    next_grad = from_behind(gated_grad[:, :reach].astype(jnp.bfloat16), "seq", -1).astype(
        jnp.float32
    )
    grad_ext = jnp.concatenate([gated_grad, next_grad], axis=1)
    conv_grad = grad_ext * query_tail
    prod_grad = correlate(conv_grad, long_filter) + skip_gain[:, None] * conv_grad[:, :keep]
    query_grad = grad_ext[:, :keep] * summed[:, :keep]
    key_grad = prod_grad * value_feat[:, taps_long - 1 : taps_long - 1 + keep]
    value_grad = prod_grad * key_feat[:, taps_long - 1 : taps_long - 1 + keep]
    feat_grad = jnp.stack([query_grad, key_grad, value_grad])
    stream_grad = short_correlate(feat_grad, feat_weight).astype(jnp.bfloat16)
    output_sum, stream_grad, weight_grad = lax.optimization_barrier(
        (output_sum, stream_grad, weight_grad)
    )
    mixed = lax.ppermute(output_sum, ("seq", "tp"), mixed_route)
    return (mixed, stream_grad, weight_grad)


def solution(mesh):
    return jax.shard_map(
        shards,
        mesh=mesh,
        in_specs=(
            P(None, "tp", "seq"),
            P(None, "tp", None),
            P("tp", None),
            P("tp"),
            P("tp", "seq"),
            P("tp", "seq"),
        ),
        out_specs=(P("tp", "seq"), P(None, "tp", "seq"), P("tp", "seq")),
        check_vma=False,
    )
```

```python
import math

import jax
import jax.numpy as jnp
from jax import lax
from jax.sharding import PartitionSpec as P


def halo(block, axis, width, short):
    count = lax.axis_size(axis)
    forward = [(i, i + 1) for i in range(count - 1)]
    backward = [(target, source) for source, target in forward]
    length = block.shape[-1]
    low = jnp.concatenate(
        [block[1, :, length - width :], block[2, :, length - width :], block[0, :, length - short :]],
        axis=-1,
    )
    high = jnp.concatenate([block[0, :, :width], block[1, :, :short], block[2, :, :short]], axis=-1)
    low = lax.ppermute(low, axis, forward)
    high = lax.ppermute(high, axis, backward)
    query = jnp.concatenate([low[:, 2 * width :], block[0], high[:, :width]], axis=-1)
    key = jnp.concatenate([low[:, :width], block[1], high[:, width : width + short]], axis=-1)
    value = jnp.concatenate(
        [low[:, width : 2 * width], block[2], high[:, width + short :]], axis=-1
    )
    return query, jnp.stack([key, value])


def from_behind(block, axis, distance):
    devices = range(lax.axis_size(axis))
    route = [(i - distance, i) for i in devices if i - distance in devices]
    return lax.ppermute(block, axis, route)


def correlate(signal, taps):
    return lax.conv_general_dilated(
        signal[None],
        taps[:, None, :],
        (1,),
        "VALID",
        dimension_numbers=("NCH", "OIH", "NCH"),
        feature_group_count=signal.shape[0],
        precision=lax.Precision.HIGHEST,
    )[0]


def short_correlate(signal, taps):
    span = signal.shape[-1] - taps.shape[-1] + 1
    total = taps[..., 0:1] * signal[..., 0:span]
    for k in range(1, taps.shape[-1]):
        total = total + taps[..., k : k + 1] * signal[..., k : k + span]
    return total


def partner(index, step, count):
    if count & (count - 1) == 0:
        return index ^ step
    return (index + step) % count


def source(index, step, count):
    if count & (count - 1) == 0:
        return index ^ step
    return (index - step) % count


def exchange(block_of, axis):
    count = lax.axis_size(axis)
    got = []
    for step in range(1, count):
        route = [(i, partner(i, step, count)) for i in range(count)]
        got.append(lax.ppermute(block_of(step), axis, route))
    return got


def rows_of_slab(out_grad, n_seq, n_tp):
    rows, length = out_grad.shape
    piece = rows // n_seq
    me = lax.axis_index("seq")
    split = out_grad.reshape(n_seq, piece, length)
    got = exchange(lambda step: split[partner(me, step, n_seq)], "seq")
    stacked = jnp.stack([split[me]] + got)
    index = jnp.zeros((n_seq,), jnp.int32)
    for step in range(1, n_seq):
        index = index + jnp.where(
            jnp.arange(n_seq) == source(me, step, n_seq), step, 0
        ).astype(jnp.int32)
    mine = jnp.take(stacked, index, axis=0)
    return jnp.transpose(mine, (1, 0, 2)).reshape(piece, n_seq * length)


def rows_gathered(mine, n_seq, n_tp):
    route = []
    for a in range(n_seq):
        for b in range(n_tp):
            flat = n_seq * b + a
            route.append((a * n_tp + b, (flat // n_tp) * n_tp + flat % n_tp))
    moved = lax.ppermute(mine, ("seq", "tp"), route)
    return lax.all_gather(moved, "tp", axis=0, tiled=True)


def shards(streams, feat_weight, long_filter, skip_gain, out_weight, out_grad):
    channels = streams.shape[1]
    length = streams.shape[2]
    taps_long = long_filter.shape[1]
    taps_short = feat_weight.shape[2]
    n_seq = lax.axis_size("seq")
    n_tp = lax.axis_size("tp")
    me = lax.axis_index("seq")
    reach = taps_long + taps_short - 2
    keep = length + taps_short - 1

    query_in, key_value_in = halo(streams, "seq", reach, taps_short - 1)
    grad_rows = lax.all_gather(out_grad, "tp", axis=0, tiled=True)
    slab_width = out_weight.shape[1]
    slab_grad = jnp.concatenate(
        [lax.dynamic_slice_in_dim(grad_rows, me * slab_width, slab_width, axis=0)]
        + exchange(
            lambda step: lax.dynamic_slice_in_dim(
                grad_rows, partner(me, step, n_seq) * slab_width, slab_width, axis=0
            ),
            "seq",
        ),
        axis=1,
    )

    key_value = short_correlate(key_value_in.astype(jnp.float32), feat_weight[1:, :, ::-1])
    key_feat, value_feat = key_value[0], key_value[1]
    query_tail = short_correlate(query_in.astype(jnp.float32), feat_weight[0, :, ::-1])
    product = key_feat * value_feat
    convolved = correlate(product, long_filter[:, ::-1])
    summed = convolved + skip_gain[:, None] * product[:, taps_long - 1 :]
    gated = (query_tail[:, :length] * summed[:, :length]).astype(jnp.bfloat16)

    gated_blocks = [gated] + exchange(lambda step: gated, "seq")
    group = n_tp // n_seq
    weight_t = out_weight.T
    pieces = [
        jnp.dot(weight_t, block, preferred_element_type=jnp.float32).astype(jnp.bfloat16)
        for block in gated_blocks
    ]
    partial_out = jnp.concatenate(pieces, axis=0)
    output_sum = lax.psum_scatter(partial_out, "tp", scatter_dimension=0, tiled=True)
    route = []
    for s in range(n_seq):
        for p in range(n_tp):
            step = p // group
            target = source(s, step, n_seq) if step else s
            route.append((s * n_tp + p, target * n_tp + group * s + p % group))
    mixed_route = route

    slab_grad, gated_blocks = lax.optimization_barrier((slab_grad, gated_blocks))
    partial_grad = jnp.dot(out_weight, slab_grad, preferred_element_type=jnp.float32)

    def relative(step):
        if n_seq & (n_seq - 1) == 0:
            return step
        return (n_seq - step) % n_seq

    def grad_block(step):
        block = partial_grad[:, relative(step) * length : (relative(step) + 1) * length]
        return block.astype(jnp.bfloat16)

    arrived = exchange(grad_block, "seq")
    gated_grad = partial_grad[:, :length]
    for block in arrived:
        gated_grad = gated_grad + block.astype(jnp.float32)

    scale = 1.0 / math.sqrt(length * n_seq)
    weight_sum = None
    for step, block in enumerate(gated_blocks):
        grad_part = slab_grad[:, step * length : (step + 1) * length]
        term = lax.dot_general(
            block, grad_part, (((1,), (1,)), ((), ())), preferred_element_type=jnp.float32
        )
        term = lax.reduce_precision(term * scale, exponent_bits=8, mantissa_bits=7)
        weight_sum = term if weight_sum is None else weight_sum + term
    weight_grad = weight_sum.astype(jnp.bfloat16)

    next_grad = from_behind(gated_grad[:, :reach].astype(jnp.bfloat16), "seq", -1).astype(
        jnp.float32
    )
    grad_ext = jnp.concatenate([gated_grad, next_grad], axis=1)
    conv_grad = grad_ext * query_tail
    prod_grad = correlate(conv_grad, long_filter) + skip_gain[:, None] * conv_grad[:, :keep]
    query_grad = grad_ext[:, :keep] * summed[:, :keep]
    key_grad = prod_grad * value_feat[:, taps_long - 1 : taps_long - 1 + keep]
    value_grad = prod_grad * key_feat[:, taps_long - 1 : taps_long - 1 + keep]
    feat_grad = jnp.stack([query_grad, key_grad, value_grad])
    stream_grad = short_correlate(feat_grad, feat_weight).astype(jnp.bfloat16)
    output_sum, stream_grad, weight_grad = lax.optimization_barrier(
        (output_sum, stream_grad, weight_grad)
    )
    mixed = lax.ppermute(output_sum, ("seq", "tp"), mixed_route)
    return (mixed, stream_grad, weight_grad)


def solution(mesh):
    return jax.shard_map(
        shards,
        mesh=mesh,
        in_specs=(
            P(None, "tp", "seq"),
            P(None, "tp", None),
            P("tp", None),
            P("tp"),
            P("tp", "seq"),
            P("tp", "seq"),
        ),
        out_specs=(P("tp", "seq"), P(None, "tp", "seq"), P("tp", "seq")),
        check_vma=False,
    )
```

```python
import math

import jax
import jax.numpy as jnp
from jax import lax
from jax.sharding import PartitionSpec as P


def halo(block, axis, width, short):
    count = lax.axis_size(axis)
    forward = [(i, i + 1) for i in range(count - 1)]
    backward = [(target, source) for source, target in forward]
    length = block.shape[-1]
    low = jnp.concatenate(
        [block[1, :, length - width :], block[2, :, length - width :], block[0, :, length - short :]],
        axis=-1,
    )
    high = jnp.concatenate([block[0, :, :width], block[1, :, :short], block[2, :, :short]], axis=-1)
    low = lax.ppermute(low, axis, forward)
    high = lax.ppermute(high, axis, backward)
    query = jnp.concatenate([low[:, 2 * width :], block[0], high[:, :width]], axis=-1)
    key = jnp.concatenate([low[:, :width], block[1], high[:, width : width + short]], axis=-1)
    value = jnp.concatenate(
        [low[:, width : 2 * width], block[2], high[:, width + short :]], axis=-1
    )
    return query, jnp.stack([key, value])


def from_behind(block, axis, distance):
    devices = range(lax.axis_size(axis))
    route = [(i - distance, i) for i in devices if i - distance in devices]
    return lax.ppermute(block, axis, route)


def correlate(signal, taps):
    return lax.conv_general_dilated(
        signal[None],
        taps[:, None, :],
        (1,),
        "VALID",
        dimension_numbers=("NCH", "OIH", "NCH"),
        feature_group_count=signal.shape[0],
        precision=lax.Precision.HIGHEST,
    )[0]


def short_correlate(signal, taps):
    span = signal.shape[-1] - taps.shape[-1] + 1
    total = taps[..., 0:1] * signal[..., 0:span]
    for k in range(1, taps.shape[-1]):
        total = total + taps[..., k : k + 1] * signal[..., k : k + span]
    return total


def partner(index, step, count):
    if count & (count - 1) == 0:
        return index ^ step
    return (index + step) % count


def source(index, step, count):
    if count & (count - 1) == 0:
        return index ^ step
    return (index - step) % count


def exchange(block_of, axis):
    count = lax.axis_size(axis)
    got = []
    for step in range(1, count):
        route = [(i, partner(i, step, count)) for i in range(count)]
        got.append(lax.ppermute(block_of(step), axis, route))
    return got


def rows_of_slab(out_grad, n_seq, n_tp):
    rows, length = out_grad.shape
    piece = rows // n_seq
    me = lax.axis_index("seq")
    split = out_grad.reshape(n_seq, piece, length)
    got = exchange(lambda step: split[partner(me, step, n_seq)], "seq")
    stacked = jnp.stack([split[me]] + got)
    index = jnp.zeros((n_seq,), jnp.int32)
    for step in range(1, n_seq):
        index = index + jnp.where(
            jnp.arange(n_seq) == source(me, step, n_seq), step, 0
        ).astype(jnp.int32)
    mine = jnp.take(stacked, index, axis=0)
    return jnp.transpose(mine, (1, 0, 2)).reshape(piece, n_seq * length)


def rows_gathered(mine, n_seq, n_tp):
    route = []
    for a in range(n_seq):
        for b in range(n_tp):
            flat = n_seq * b + a
            route.append((a * n_tp + b, (flat // n_tp) * n_tp + flat % n_tp))
    moved = lax.ppermute(mine, ("seq", "tp"), route)
    return lax.all_gather(moved, "tp", axis=0, tiled=True)


def shards(streams, feat_weight, long_filter, skip_gain, out_weight, out_grad):
    channels = streams.shape[1]
    length = streams.shape[2]
    taps_long = long_filter.shape[1]
    taps_short = feat_weight.shape[2]
    n_seq = lax.axis_size("seq")
    n_tp = lax.axis_size("tp")
    me = lax.axis_index("seq")
    reach = taps_long + taps_short - 2
    keep = length + taps_short - 1

    slab_piece = rows_of_slab(out_grad, n_seq, n_tp)
    streams, slab_piece = lax.optimization_barrier((streams, slab_piece))
    query_in, key_value_in = halo(streams, "seq", reach, taps_short - 1)
    slab_grad = rows_gathered(slab_piece, n_seq, n_tp)
    slab_width = slab_grad.shape[0]

    key_value = short_correlate(key_value_in.astype(jnp.float32), feat_weight[1:, :, ::-1])
    key_feat, value_feat = key_value[0], key_value[1]
    query_tail = short_correlate(query_in.astype(jnp.float32), feat_weight[0, :, ::-1])
    product = key_feat * value_feat
    convolved = correlate(product, long_filter[:, ::-1])
    summed = convolved + skip_gain[:, None] * product[:, taps_long - 1 :]
    gated = (query_tail[:, :length] * summed[:, :length]).astype(jnp.bfloat16)

    gated_blocks = [gated] + exchange(lambda step: gated, "seq")
    group = n_tp // n_seq
    weight_t = out_weight.T
    partial_out = jnp.zeros((n_seq * slab_width, length), jnp.bfloat16)
    for m, block in enumerate(gated_blocks):
        piece = jnp.dot(weight_t, block, preferred_element_type=jnp.float32).astype(jnp.bfloat16)
        partial_out = lax.dynamic_update_slice_in_dim(partial_out, piece, m * slab_width, axis=0)
    output_sum = lax.psum_scatter(partial_out, "tp", scatter_dimension=0, tiled=True)
    route = []
    for s in range(n_seq):
        for p in range(n_tp):
            step = p // group
            target = source(s, step, n_seq) if step else s
            route.append((s * n_tp + p, target * n_tp + group * s + p % group))
    mixed_route = route

    slab_grad, gated_blocks = lax.optimization_barrier((slab_grad, gated_blocks))
    partial_grad = jnp.dot(out_weight, slab_grad, preferred_element_type=jnp.float32)

    def grad_block(step):
        start = partner(me, step, n_seq) * length
        block = lax.dynamic_slice_in_dim(partial_grad, start, length, axis=1)
        return block.astype(jnp.bfloat16)

    arrived = exchange(grad_block, "seq")
    gated_grad = lax.dynamic_slice_in_dim(partial_grad, me * length, length, axis=1)
    for block in arrived:
        gated_grad = gated_grad + block.astype(jnp.float32)

    scale = 1.0 / math.sqrt(length * n_seq)
    weight_sum = None
    for step, block in enumerate(gated_blocks):
        origin = source(me, step, n_seq) if step else me
        grad_part = lax.dynamic_slice_in_dim(slab_grad, origin * length, length, axis=1)
        term = lax.dot_general(
            block, grad_part, (((1,), (1,)), ((), ())), preferred_element_type=jnp.float32
        )
        term = lax.reduce_precision(term * scale, exponent_bits=8, mantissa_bits=7)
        weight_sum = term if weight_sum is None else weight_sum + term
    weight_grad = weight_sum.astype(jnp.bfloat16)

    next_grad = from_behind(gated_grad[:, :reach].astype(jnp.bfloat16), "seq", -1).astype(
        jnp.float32
    )
    grad_ext = jnp.concatenate([gated_grad, next_grad], axis=1)
    conv_grad = grad_ext * query_tail
    prod_grad = correlate(conv_grad, long_filter) + skip_gain[:, None] * conv_grad[:, :keep]
    query_grad = grad_ext[:, :keep] * summed[:, :keep]
    key_grad = prod_grad * value_feat[:, taps_long - 1 : taps_long - 1 + keep]
    value_grad = prod_grad * key_feat[:, taps_long - 1 : taps_long - 1 + keep]
    feat_grad = jnp.stack([query_grad, key_grad, value_grad])
    stream_grad = short_correlate(feat_grad, feat_weight).astype(jnp.bfloat16)
    output_sum, stream_grad, weight_grad = lax.optimization_barrier(
        (output_sum, stream_grad, weight_grad)
    )
    mixed = lax.ppermute(output_sum, ("seq", "tp"), mixed_route)
    return (mixed, stream_grad, weight_grad)


def solution(mesh):
    return jax.shard_map(
        shards,
        mesh=mesh,
        in_specs=(
            P(None, "tp", "seq"),
            P(None, "tp", None),
            P("tp", None),
            P("tp"),
            P("tp", "seq"),
            P("tp", "seq"),
        ),
        out_specs=(P("tp", "seq"), P(None, "tp", "seq"), P("tp", "seq")),
        check_vma=False,
    )
```

```python
import math

import jax
import jax.numpy as jnp
from jax import lax
from jax.experimental.layout import Layout, with_layout_constraint
from jax.sharding import PartitionSpec as P


def halo(block, axis, width, short):
    count = lax.axis_size(axis)
    forward = [(i, i + 1) for i in range(count - 1)]
    backward = [(target, source) for source, target in forward]
    length = block.shape[-1]
    low = jnp.concatenate(
        [block[1, :, length - width :], block[2, :, length - width :], block[0, :, length - short :]],
        axis=-1,
    )
    high = jnp.concatenate([block[0, :, :width], block[1, :, :short], block[2, :, :short]], axis=-1)
    low = lax.ppermute(low, axis, forward)
    high = lax.ppermute(high, axis, backward)
    query = jnp.concatenate([low[:, 2 * width :], block[0], high[:, :width]], axis=-1)
    key = jnp.concatenate([low[:, :width], block[1], high[:, width : width + short]], axis=-1)
    value = jnp.concatenate(
        [low[:, width : 2 * width], block[2], high[:, width + short :]], axis=-1
    )
    return query, jnp.stack([key, value])


def from_behind(block, axis, distance):
    devices = range(lax.axis_size(axis))
    route = [(i - distance, i) for i in devices if i - distance in devices]
    return lax.ppermute(block, axis, route)


def correlate(signal, taps):
    return lax.conv_general_dilated(
        signal[None],
        taps[:, None, :],
        (1,),
        "VALID",
        dimension_numbers=("NCH", "OIH", "NCH"),
        feature_group_count=signal.shape[0],
        precision=lax.Precision.HIGHEST,
    )[0]


def short_correlate(signal, taps):
    span = signal.shape[-1] - taps.shape[-1] + 1
    total = taps[..., 0:1] * signal[..., 0:span]
    for k in range(1, taps.shape[-1]):
        total = total + taps[..., k : k + 1] * signal[..., k : k + span]
    return total


def partner(index, step, count):
    if count & (count - 1) == 0:
        return index ^ step
    return (index + step) % count


def source(index, step, count):
    if count & (count - 1) == 0:
        return index ^ step
    return (index - step) % count


def exchange(block_of, axis):
    count = lax.axis_size(axis)
    got = []
    for step in range(1, count):
        route = [(i, partner(i, step, count)) for i in range(count)]
        got.append(lax.ppermute(block_of(step), axis, route))
    return got


def rows_of_slab(out_grad, n_seq, n_tp):
    rows, length = out_grad.shape
    piece = rows // n_seq
    me = lax.axis_index("seq")
    split = out_grad.reshape(n_seq, piece, length)
    got = exchange(lambda step: split[partner(me, step, n_seq)], "seq")
    stacked = jnp.stack([split[me]] + got)
    index = jnp.zeros((n_seq,), jnp.int32)
    for step in range(1, n_seq):
        index = index + jnp.where(
            jnp.arange(n_seq) == source(me, step, n_seq), step, 0
        ).astype(jnp.int32)
    mine = jnp.take(stacked, index, axis=0)
    return jnp.transpose(mine, (1, 0, 2)).reshape(piece, n_seq * length)


def rows_gathered(mine, n_seq, n_tp):
    route = []
    for a in range(n_seq):
        for b in range(n_tp):
            flat = n_seq * b + a
            route.append((a * n_tp + b, (flat // n_tp) * n_tp + flat % n_tp))
    moved = lax.ppermute(mine, ("seq", "tp"), route)
    return lax.all_gather(moved, "tp", axis=0, tiled=True)


def shards(streams, feat_weight, long_filter, skip_gain, out_weight, out_grad):
    channels = streams.shape[1]
    length = streams.shape[2]
    taps_long = long_filter.shape[1]
    taps_short = feat_weight.shape[2]
    n_seq = lax.axis_size("seq")
    n_tp = lax.axis_size("tp")
    me = lax.axis_index("seq")
    reach = taps_long + taps_short - 2
    keep = length + taps_short - 1

    slab_piece = rows_of_slab(out_grad, n_seq, n_tp)
    streams, slab_piece = lax.optimization_barrier((streams, slab_piece))
    query_in, key_value_in = halo(streams, "seq", reach, taps_short - 1)
    slab_grad = rows_gathered(slab_piece, n_seq, n_tp)
    slab_width = slab_grad.shape[0]

    key_value = short_correlate(key_value_in.astype(jnp.float32), feat_weight[1:, :, ::-1])
    key_feat, value_feat = key_value[0], key_value[1]
    query_tail = short_correlate(query_in.astype(jnp.float32), feat_weight[0, :, ::-1])
    product = key_feat * value_feat
    convolved = correlate(product, long_filter[:, ::-1])
    summed = convolved + skip_gain[:, None] * product[:, taps_long - 1 :]
    gated = (query_tail[:, :length] * summed[:, :length]).astype(jnp.bfloat16)

    gated_blocks = [gated] + exchange(lambda step: gated, "seq")
    group = n_tp // n_seq
    weight_t = out_weight.T
    pieces = [
        jnp.dot(weight_t, block, preferred_element_type=jnp.float32).astype(jnp.bfloat16)
        for block in gated_blocks
    ]
    partial_out = jnp.concatenate(pieces, axis=0)
    partial_out = with_layout_constraint(partial_out, Layout(major_to_minor=(0, 1)))
    output_sum = lax.psum_scatter(partial_out, "tp", scatter_dimension=0, tiled=True)
    route = []
    for s in range(n_seq):
        for p in range(n_tp):
            step = p // group
            target = source(s, step, n_seq) if step else s
            route.append((s * n_tp + p, target * n_tp + group * s + p % group))
    mixed_route = route

    slab_grad, gated_blocks = lax.optimization_barrier((slab_grad, gated_blocks))
    partial_grad = jnp.dot(out_weight, slab_grad, preferred_element_type=jnp.float32)

    def grad_block(step):
        start = partner(me, step, n_seq) * length
        block = lax.dynamic_slice_in_dim(partial_grad, start, length, axis=1)
        return block.astype(jnp.bfloat16)

    arrived = exchange(grad_block, "seq")
    gated_grad = lax.dynamic_slice_in_dim(partial_grad, me * length, length, axis=1)
    for block in arrived:
        gated_grad = gated_grad + block.astype(jnp.float32)

    scale = 1.0 / math.sqrt(length * n_seq)
    weight_sum = None
    for step, block in enumerate(gated_blocks):
        origin = source(me, step, n_seq) if step else me
        grad_part = lax.dynamic_slice_in_dim(slab_grad, origin * length, length, axis=1)
        term = lax.dot_general(
            block, grad_part, (((1,), (1,)), ((), ())), preferred_element_type=jnp.float32
        )
        term = lax.reduce_precision(term * scale, exponent_bits=8, mantissa_bits=7)
        weight_sum = term if weight_sum is None else weight_sum + term
    weight_grad = weight_sum.astype(jnp.bfloat16)

    next_grad = from_behind(gated_grad[:, :reach].astype(jnp.bfloat16), "seq", -1).astype(
        jnp.float32
    )
    grad_ext = jnp.concatenate([gated_grad, next_grad], axis=1)
    conv_grad = grad_ext * query_tail
    prod_grad = correlate(conv_grad, long_filter) + skip_gain[:, None] * conv_grad[:, :keep]
    query_grad = grad_ext[:, :keep] * summed[:, :keep]
    key_grad = prod_grad * value_feat[:, taps_long - 1 : taps_long - 1 + keep]
    value_grad = prod_grad * key_feat[:, taps_long - 1 : taps_long - 1 + keep]
    feat_grad = jnp.stack([query_grad, key_grad, value_grad])
    stream_grad = short_correlate(feat_grad, feat_weight).astype(jnp.bfloat16)
    output_sum, stream_grad, weight_grad = lax.optimization_barrier(
        (output_sum, stream_grad, weight_grad)
    )
    mixed = lax.ppermute(output_sum, ("seq", "tp"), mixed_route)
    return (mixed, stream_grad, weight_grad)


def solution(mesh):
    return jax.shard_map(
        shards,
        mesh=mesh,
        in_specs=(
            P(None, "tp", "seq"),
            P(None, "tp", None),
            P("tp", None),
            P("tp"),
            P("tp", "seq"),
            P("tp", "seq"),
        ),
        out_specs=(P("tp", "seq"), P(None, "tp", "seq"), P("tp", "seq")),
        check_vma=False,
    )
```

```python
import math

import jax
import jax.numpy as jnp
from jax import lax
from jax.sharding import PartitionSpec as P


def halo(block, axis, width, short):
    count = lax.axis_size(axis)
    forward = [(i, i + 1) for i in range(count - 1)]
    backward = [(target, source) for source, target in forward]
    length = block.shape[-1]
    low = jnp.concatenate(
        [block[1, :, length - width :], block[2, :, length - width :], block[0, :, length - short :]],
        axis=-1,
    )
    high = jnp.concatenate([block[0, :, :width], block[1, :, :short], block[2, :, :short]], axis=-1)
    low = lax.ppermute(low, axis, forward)
    high = lax.ppermute(high, axis, backward)
    query_head = jnp.concatenate([low[:, 2 * width :], block[0]], axis=-1)
    key_value_head = jnp.stack(
        [
            jnp.concatenate([low[:, :width], block[1]], axis=-1),
            jnp.concatenate([low[:, width : 2 * width], block[2]], axis=-1),
        ]
    )
    query = jnp.concatenate([query_head, high[:, :width]], axis=-1)
    key = jnp.concatenate([key_value_head[0], high[:, width : width + short]], axis=-1)
    value = jnp.concatenate([key_value_head[1], high[:, width + short :]], axis=-1)
    return query_head, key_value_head, query, jnp.stack([key, value])


def from_behind(block, axis, distance):
    devices = range(lax.axis_size(axis))
    route = [(i - distance, i) for i in devices if i - distance in devices]
    return lax.ppermute(block, axis, route)


def correlate(signal, taps):
    return lax.conv_general_dilated(
        signal[None],
        taps[:, None, :],
        (1,),
        "VALID",
        dimension_numbers=("NCH", "OIH", "NCH"),
        feature_group_count=signal.shape[0],
        precision=lax.Precision.HIGHEST,
    )[0]


def short_correlate(signal, taps):
    span = signal.shape[-1] - taps.shape[-1] + 1
    total = taps[..., 0:1] * signal[..., 0:span]
    for k in range(1, taps.shape[-1]):
        total = total + taps[..., k : k + 1] * signal[..., k : k + span]
    return total


def partner(index, step, count):
    if count & (count - 1) == 0:
        return index ^ step
    return (index + step) % count


def source(index, step, count):
    if count & (count - 1) == 0:
        return index ^ step
    return (index - step) % count


def exchange(block_of, axis):
    count = lax.axis_size(axis)
    got = []
    for step in range(1, count):
        route = [(i, partner(i, step, count)) for i in range(count)]
        got.append(lax.ppermute(block_of(step), axis, route))
    return got


def rows_of_slab(out_grad, n_seq, n_tp):
    rows, length = out_grad.shape
    piece = rows // n_seq
    me = lax.axis_index("seq")
    split = out_grad.reshape(n_seq, piece, length)
    got = exchange(lambda step: split[partner(me, step, n_seq)], "seq")
    stacked = jnp.stack([split[me]] + got)
    index = jnp.zeros((n_seq,), jnp.int32)
    for step in range(1, n_seq):
        index = index + jnp.where(
            jnp.arange(n_seq) == source(me, step, n_seq), step, 0
        ).astype(jnp.int32)
    mine = jnp.take(stacked, index, axis=0)
    return jnp.transpose(mine, (1, 0, 2)).reshape(piece, n_seq * length)


def rows_gathered(mine, n_seq, n_tp):
    route = []
    for a in range(n_seq):
        for b in range(n_tp):
            flat = n_seq * b + a
            route.append((a * n_tp + b, (flat // n_tp) * n_tp + flat % n_tp))
    moved = lax.ppermute(mine, ("seq", "tp"), route)
    return lax.all_gather(moved, "tp", axis=0, tiled=True)


def shards(streams, feat_weight, long_filter, skip_gain, out_weight, out_grad):
    channels = streams.shape[1]
    length = streams.shape[2]
    taps_long = long_filter.shape[1]
    taps_short = feat_weight.shape[2]
    n_seq = lax.axis_size("seq")
    n_tp = lax.axis_size("tp")
    me = lax.axis_index("seq")
    reach = taps_long + taps_short - 2
    keep = length + taps_short - 1

    slab_piece = rows_of_slab(out_grad, n_seq, n_tp)
    streams, slab_piece = lax.optimization_barrier((streams, slab_piece))
    query_head_in, key_value_head_in, query_in, key_value_in = halo(
        streams, "seq", reach, taps_short - 1
    )
    slab_grad = rows_gathered(slab_piece, n_seq, n_tp)
    slab_width = slab_grad.shape[0]

    key_value_head = short_correlate(
        key_value_head_in.astype(jnp.float32), feat_weight[1:, :, ::-1]
    )
    query_head = short_correlate(query_head_in.astype(jnp.float32), feat_weight[0, :, ::-1])
    product_head = key_value_head[0] * key_value_head[1]
    summed_head = correlate(product_head, long_filter[:, ::-1]) + (
        skip_gain[:, None] * product_head[:, taps_long - 1 :]
    )
    gated = (query_head * summed_head).astype(jnp.bfloat16)

    gated_blocks = [gated] + exchange(lambda step: gated, "seq")
    group = n_tp // n_seq
    weight_t = out_weight.T
    partial_out = jnp.zeros((n_seq * slab_width, length), jnp.bfloat16)
    for m, block in enumerate(gated_blocks):
        piece = jnp.dot(weight_t, block, preferred_element_type=jnp.float32).astype(jnp.bfloat16)
        partial_out = lax.dynamic_update_slice_in_dim(partial_out, piece, m * slab_width, axis=0)
    output_sum = lax.psum_scatter(partial_out, "tp", scatter_dimension=0, tiled=True)
    route = []
    for s in range(n_seq):
        for p in range(n_tp):
            step = p // group
            target = source(s, step, n_seq) if step else s
            route.append((s * n_tp + p, target * n_tp + group * s + p % group))
    mixed_route = route

    key_value = short_correlate(key_value_in.astype(jnp.float32), feat_weight[1:, :, ::-1])
    key_feat, value_feat = key_value[0], key_value[1]
    query_tail = short_correlate(query_in.astype(jnp.float32), feat_weight[0, :, ::-1])
    product = key_feat * value_feat
    past = product[:, length:]
    summed_next = correlate(past, long_filter[:, ::-1]) + (
        skip_gain[:, None] * past[:, taps_long - 1 :]
    )
    summed = jnp.concatenate([summed_head, summed_next], axis=1)

    slab_grad, gated_blocks = lax.optimization_barrier((slab_grad, gated_blocks))
    partial_grad = jnp.dot(out_weight, slab_grad, preferred_element_type=jnp.float32)

    def grad_block(step):
        start = partner(me, step, n_seq) * length
        block = lax.dynamic_slice_in_dim(partial_grad, start, length, axis=1)
        return block.astype(jnp.bfloat16)

    arrived = exchange(grad_block, "seq")
    gated_grad = lax.dynamic_slice_in_dim(partial_grad, me * length, length, axis=1)
    for block in arrived:
        gated_grad = gated_grad + block.astype(jnp.float32)

    scale = 1.0 / math.sqrt(length * n_seq)
    weight_sum = None
    for step, block in enumerate(gated_blocks):
        origin = source(me, step, n_seq) if step else me
        grad_part = lax.dynamic_slice_in_dim(slab_grad, origin * length, length, axis=1)
        term = lax.dot_general(
            block, grad_part, (((1,), (1,)), ((), ())), preferred_element_type=jnp.float32
        )
        term = lax.reduce_precision(term * scale, exponent_bits=8, mantissa_bits=7)
        weight_sum = term if weight_sum is None else weight_sum + term
    weight_grad = weight_sum.astype(jnp.bfloat16)

    next_grad = from_behind(gated_grad[:, :reach].astype(jnp.bfloat16), "seq", -1).astype(
        jnp.float32
    )
    grad_ext = jnp.concatenate([gated_grad, next_grad], axis=1)
    conv_grad = grad_ext * query_tail
    prod_grad = correlate(conv_grad, long_filter) + skip_gain[:, None] * conv_grad[:, :keep]
    query_grad = grad_ext[:, :keep] * summed[:, :keep]
    key_grad = prod_grad * value_feat[:, taps_long - 1 : taps_long - 1 + keep]
    value_grad = prod_grad * key_feat[:, taps_long - 1 : taps_long - 1 + keep]
    feat_grad = jnp.stack([query_grad, key_grad, value_grad])
    stream_grad = short_correlate(feat_grad, feat_weight).astype(jnp.bfloat16)
    output_sum, stream_grad, weight_grad = lax.optimization_barrier(
        (output_sum, stream_grad, weight_grad)
    )
    mixed = lax.ppermute(output_sum, ("seq", "tp"), mixed_route)
    return (mixed, stream_grad, weight_grad)


def solution(mesh):
    return jax.shard_map(
        shards,
        mesh=mesh,
        in_specs=(
            P(None, "tp", "seq"),
            P(None, "tp", None),
            P("tp", None),
            P("tp"),
            P("tp", "seq"),
            P("tp", "seq"),
        ),
        out_specs=(P("tp", "seq"), P(None, "tp", "seq"), P("tp", "seq")),
        check_vma=False,
    )
```

```python
import math

import jax
import jax.numpy as jnp
from jax import lax
from jax.experimental.layout import Layout, with_layout_constraint
from jax.sharding import PartitionSpec as P


def halo(block, axis, width, short):
    count = lax.axis_size(axis)
    forward = [(i, i + 1) for i in range(count - 1)]
    backward = [(target, source) for source, target in forward]
    length = block.shape[-1]
    low = jnp.concatenate(
        [block[1, :, length - width :], block[2, :, length - width :], block[0, :, length - short :]],
        axis=-1,
    )
    high = jnp.concatenate([block[0, :, :width], block[1, :, :short], block[2, :, :short]], axis=-1)
    low = lax.ppermute(low, axis, forward)
    high = lax.ppermute(high, axis, backward)
    query = jnp.concatenate([low[:, 2 * width :], block[0], high[:, :width]], axis=-1)
    key = jnp.concatenate([low[:, :width], block[1], high[:, width : width + short]], axis=-1)
    value = jnp.concatenate(
        [low[:, width : 2 * width], block[2], high[:, width + short :]], axis=-1
    )
    return query, jnp.stack([key, value])


def from_behind(block, axis, distance):
    devices = range(lax.axis_size(axis))
    route = [(i - distance, i) for i in devices if i - distance in devices]
    return lax.ppermute(block, axis, route)


def correlate(signal, taps):
    return lax.conv_general_dilated(
        signal[None],
        taps[:, None, :],
        (1,),
        "VALID",
        dimension_numbers=("NCH", "OIH", "NCH"),
        feature_group_count=signal.shape[0],
        precision=lax.Precision.HIGHEST,
    )[0]


def short_correlate(signal, taps):
    span = signal.shape[-1] - taps.shape[-1] + 1
    total = taps[..., 0:1] * signal[..., 0:span]
    for k in range(1, taps.shape[-1]):
        total = total + taps[..., k : k + 1] * signal[..., k : k + span]
    return total


def partner(index, step, count):
    if count & (count - 1) == 0:
        return index ^ step
    return (index + step) % count


def source(index, step, count):
    if count & (count - 1) == 0:
        return index ^ step
    return (index - step) % count


def exchange(block_of, axis):
    count = lax.axis_size(axis)
    got = []
    for step in range(1, count):
        route = [(i, partner(i, step, count)) for i in range(count)]
        got.append(lax.ppermute(block_of(step), axis, route))
    return got


def rows_of_slab(out_grad, n_seq, n_tp):
    rows, length = out_grad.shape
    piece = rows // n_seq
    me = lax.axis_index("seq")
    split = out_grad.reshape(n_seq, piece, length)
    got = exchange(lambda step: split[partner(me, step, n_seq)], "seq")
    stacked = jnp.stack([split[me]] + got)
    index = jnp.zeros((n_seq,), jnp.int32)
    for step in range(1, n_seq):
        index = index + jnp.where(
            jnp.arange(n_seq) == source(me, step, n_seq), step, 0
        ).astype(jnp.int32)
    mine = jnp.take(stacked, index, axis=0)
    return jnp.transpose(mine, (1, 0, 2)).reshape(piece, n_seq * length)


def rows_gathered(mine, n_seq, n_tp):
    route = []
    for a in range(n_seq):
        for b in range(n_tp):
            flat = n_seq * b + a
            route.append((a * n_tp + b, (flat // n_tp) * n_tp + flat % n_tp))
    moved = lax.ppermute(mine, ("seq", "tp"), route)
    moved = with_layout_constraint(moved, Layout(major_to_minor=(0, 1)))
    gathered = lax.all_gather(moved, "tp", axis=0, tiled=True)
    return with_layout_constraint(gathered, Layout(major_to_minor=(0, 1)))


def shards(streams, feat_weight, long_filter, skip_gain, out_weight, out_grad):
    channels = streams.shape[1]
    length = streams.shape[2]
    taps_long = long_filter.shape[1]
    taps_short = feat_weight.shape[2]
    n_seq = lax.axis_size("seq")
    n_tp = lax.axis_size("tp")
    me = lax.axis_index("seq")
    reach = taps_long + taps_short - 2
    keep = length + taps_short - 1

    slab_piece = rows_of_slab(out_grad, n_seq, n_tp)
    streams, slab_piece = lax.optimization_barrier((streams, slab_piece))
    query_in, key_value_in = halo(streams, "seq", reach, taps_short - 1)
    slab_grad = rows_gathered(slab_piece, n_seq, n_tp)
    slab_width = slab_grad.shape[0]

    key_value = short_correlate(key_value_in.astype(jnp.float32), feat_weight[1:, :, ::-1])
    key_feat, value_feat = key_value[0], key_value[1]
    query_tail = short_correlate(query_in.astype(jnp.float32), feat_weight[0, :, ::-1])
    product = key_feat * value_feat
    convolved = correlate(product, long_filter[:, ::-1])
    summed = convolved + skip_gain[:, None] * product[:, taps_long - 1 :]
    gated = (query_tail[:, :length] * summed[:, :length]).astype(jnp.bfloat16)

    gated_blocks = [gated] + exchange(lambda step: gated, "seq")
    group = n_tp // n_seq
    weight_t = out_weight.T
    pieces = [
        jnp.dot(weight_t, block, preferred_element_type=jnp.float32).astype(jnp.bfloat16)
        for block in gated_blocks
    ]
    partial_out = jnp.concatenate(pieces, axis=0)
    output_sum = lax.psum_scatter(partial_out, "tp", scatter_dimension=0, tiled=True)
    route = []
    for s in range(n_seq):
        for p in range(n_tp):
            step = p // group
            target = source(s, step, n_seq) if step else s
            route.append((s * n_tp + p, target * n_tp + group * s + p % group))
    mixed_route = route

    slab_grad, gated_blocks = lax.optimization_barrier((slab_grad, gated_blocks))
    partial_grad = jnp.dot(out_weight, slab_grad, preferred_element_type=jnp.float32)

    def grad_block(step):
        start = partner(me, step, n_seq) * length
        block = lax.dynamic_slice_in_dim(partial_grad, start, length, axis=1)
        return block.astype(jnp.bfloat16)

    arrived = exchange(grad_block, "seq")
    gated_grad = lax.dynamic_slice_in_dim(partial_grad, me * length, length, axis=1)
    for block in arrived:
        gated_grad = gated_grad + block.astype(jnp.float32)

    scale = 1.0 / math.sqrt(length * n_seq)
    weight_sum = None
    for step, block in enumerate(gated_blocks):
        origin = source(me, step, n_seq) if step else me
        grad_part = lax.dynamic_slice_in_dim(slab_grad, origin * length, length, axis=1)
        term = lax.dot_general(
            block, grad_part, (((1,), (1,)), ((), ())), preferred_element_type=jnp.float32
        )
        term = lax.reduce_precision(term * scale, exponent_bits=8, mantissa_bits=7)
        weight_sum = term if weight_sum is None else weight_sum + term
    weight_grad = weight_sum.astype(jnp.bfloat16)

    next_grad = from_behind(gated_grad[:, :reach].astype(jnp.bfloat16), "seq", -1).astype(
        jnp.float32
    )
    grad_ext = jnp.concatenate([gated_grad, next_grad], axis=1)
    conv_grad = grad_ext * query_tail
    prod_grad = correlate(conv_grad, long_filter) + skip_gain[:, None] * conv_grad[:, :keep]
    query_grad = grad_ext[:, :keep] * summed[:, :keep]
    key_grad = prod_grad * value_feat[:, taps_long - 1 : taps_long - 1 + keep]
    value_grad = prod_grad * key_feat[:, taps_long - 1 : taps_long - 1 + keep]
    feat_grad = jnp.stack([query_grad, key_grad, value_grad])
    stream_grad = short_correlate(feat_grad, feat_weight).astype(jnp.bfloat16)
    output_sum, stream_grad, weight_grad = lax.optimization_barrier(
        (output_sum, stream_grad, weight_grad)
    )
    mixed = lax.ppermute(output_sum, ("seq", "tp"), mixed_route)
    return (mixed, stream_grad, weight_grad)


def solution(mesh):
    return jax.shard_map(
        shards,
        mesh=mesh,
        in_specs=(
            P(None, "tp", "seq"),
            P(None, "tp", None),
            P("tp", None),
            P("tp"),
            P("tp", "seq"),
            P("tp", "seq"),
        ),
        out_specs=(P("tp", "seq"), P(None, "tp", "seq"), P("tp", "seq")),
        check_vma=False,
    )
```
